32 devices in a mesh: grp: 2 (over y), resp: 16 (over z, x, core).
Axes of the slice: x: 2, y: 2, z: 4, core: 2. Of those that a mesh axis runs over, the one named last changes fastest.
Arguments:
- queries: bfloat16 [4096, 2560], P(('grp', 'resp')), parts along dimension 0, may hold values from -120 to 120
- response_keys: bfloat16 [4096, 512], P(('grp', 'resp')), parts along dimension 0, may hold values from -6 to 6
- response_values: bfloat16 [4096, 512], P(('grp', 'resp')), parts along dimension 0, may hold values from -6 to 6
- document_keys: bfloat16 [256, 512], P(('grp', 'resp')), parts along dimension 0, may hold values from -6 to 6
- document_values: bfloat16 [256, 512], P(('grp', 'resp')), parts along dimension 0, may hold values from -6 to 6
- grad_out: bfloat16 [4096, 2560], P(('grp', 'resp')), parts along dimension 0, may hold values from -6 to 6
- lengths: int32 [64], P(('grp', 'resp')), parts along dimension 0, may hold values from 1 to 64, 1280 in all
- doc_mask: int32 [64, 16], P(('grp', 'resp')), parts along dimension 0, may hold values 0 or 1
Outputs:
- query_gradient: bfloat16 [4096, 2560], P(('grp', 'resp')), parts along dimension 0
- grad_doc_keys: bfloat16 [256, 512], P(('grp', 'resp')), parts along dimension 0
- grad_doc_values: bfloat16 [256, 512], P(('grp', 'resp')), parts along dimension 0
- grad_resp_keys: bfloat16 [4096, 512], P(('grp', 'resp')), parts along dimension 0
- grad_resp_values: bfloat16 [4096, 512], P(('grp', 'resp')), parts along dimension 0
The draws below stay inside these ranges and needn't reach their ends.
There are 2 independent parts, one for each index of `grp`. The reference program is written for one: setup_inputs(seed, part) draws one part's arguments, and reference() takes and returns one part's arrays. A program takes and returns all parts, laid end to end along the dimension named above; each array names one. Nothing has to cross between parts.
All inputs are finite; a program needn't handle non-finite values. No bound on the sum of `lengths` or of `doc_mask` on one device may be relied on, other than what follows from the above.
Results may differ from the reference program's by a relative error of at most 0.0051.
Values may be sent and summed in bfloat16 or wider, within the bound.
No kernel may reach another device: no remote copies, remote signals or barrier semaphores. Data moves between devices by JAX's collectives and lax.ppermute only.
A program may use at most 64 MiB of HBM per device.

```python
import math
import jax
import jax.numpy as jnp
import numpy as np
from jax import lax

KEY_HEADS = 4
GROUP_HEADS = 5
HEAD_SIZE = 128
RESPONSE_LENGTH = 64
SLAB = 8
QUERY_HEADS = 20
GROUP_RESPONSES = 32
GROUP_TOKENS = 2048
DOCUMENT_ROWS = 128
NBLK = 16


def document_base(key):
    start_offset = jnp.clip(jax.random.normal(jax.random.fold_in(key, 7), (DOCUMENT_ROWS, KEY_HEADS * HEAD_SIZE), jnp.float32), -6.0, 6.0)
    return start_offset


def draw_document_keys(key, part):
    return document_base(key).astype(jnp.bfloat16)


def draw_queries(key, part):
    start_offset = jnp.clip(jax.random.normal(jax.random.fold_in(key, 13), (GROUP_TOKENS, QUERY_HEADS * HEAD_SIZE), jnp.float32), -6.0, 6.0)
    return start_offset.astype(jnp.bfloat16)


def touch_ends(values, rng, low, top_value):
    longest = values.shape.index(max(values.shape))
    spots = []
    for shift in (0, 1):
        where = [jax.random.randint(jax.random.fold_in(rng, axis), (), 0, length) for axis, length in enumerate(values.shape)]
        where[longest] = (where[longest] + shift) % values.shape[longest]
        spots.append(tuple(where))
    return values.at[spots[0]].set(low).at[spots[1]].set(top_value)


def level_of(key, extent, cuts, smallest, largest):
    def one(dim, parts):
        steps = jax.random.uniform(jax.random.fold_in(jax.random.fold_in(key, 6), dim), (parts,), jnp.float32, smallest / len(cuts), largest / len(cuts))
        return jnp.repeat(jnp.exp(steps), extent[dim] // parts).reshape((-1,) + (1,) * (len(extent) - dim - 1))

    level = one(*cuts[0])
    for cut in cuts[1:]:
        level = level * one(*cut)
    return level


def split_up(amount, total, bound, lean):
    weights = [(1 << 20) // math.isqrt(rank ** lean) + 1 for rank in range(2, amount + 1)]
    spare, counts = total - bound - (amount - 1), [1] * (amount - 1)
    while spare > 0:
        candidates = [i for i in range(amount - 1) if counts[i] < bound]
        pool, remaining = sum([weights[i] for i in candidates]), spare
        for i in candidates:
            addition = min(bound - counts[i], max(1, remaining * weights[i] // pool), spare)
            counts[i] = counts[i] + addition
            spare = spare - addition
    return np.array([bound] + counts)


def ragged_sizes(stream_key, count, total, limit, skew):
    if count == 2:
        one = jax.random.randint(stream_key, (), max(1, total - limit), min(limit, total - 1) + 1)
        return jnp.stack([one, total - one])
    tallies = jnp.asarray(split_up(count, total, limit, skew), jnp.int32)
    twos = (count - 1) // 2
    source_of, taker = tallies[1:1 + 2 * twos:2], tallies[2:2 + 2 * twos:2]
    margin = jnp.minimum(source_of - 1, limit - taker)
    passed = jax.random.randint(jax.random.fold_in(stream_key, 1), (twos,), 0, 1 << 20) % (margin + 1)
    tallies = tallies.at[1:1 + 2 * twos:2].set(source_of - passed).at[2:2 + 2 * twos:2].set(taker + passed)
    return tallies[jax.random.permutation(jax.random.fold_in(stream_key, 2), count)]


def bell_draw(rng, extent, deviation, limit, pieces=(), kind=jnp.bfloat16):
    result = jax.random.normal(rng, extent, jnp.float32) * deviation
    if len(pieces) > 0:
        result = level_of(rng, extent, pieces, -0.22, 0.18) * result
    return jnp.clip(result, min=-limit, max=limit).astype(kind)


def setup_inputs(seed: int = 0, part: int = 0) -> dict:
    splits = jax.random.split(jax.random.key(seed), 9)
    part_splits = jax.random.split(jax.random.fold_in(splits[8], part), 9)
    return {
        "queries": draw_queries(jax.random.fold_in(jax.random.fold_in(splits[8], part), 71), part),
        "response_keys": bell_draw(part_splits[1], (GROUP_TOKENS, KEY_HEADS * HEAD_SIZE), 1.0, 6.0, ((0, 16),)),
        "response_values": bell_draw(part_splits[2], (GROUP_TOKENS, KEY_HEADS * HEAD_SIZE), 1.0, 6.0, ((0, 16),)),
        "document_keys": draw_document_keys(jax.random.fold_in(jax.random.fold_in(splits[8], part), 71), part),
        "document_values": bell_draw(part_splits[4], (DOCUMENT_ROWS, KEY_HEADS * HEAD_SIZE), 1.0, 6.0, ((0, 16),)),
        "grad_out": bell_draw(part_splits[5], (GROUP_TOKENS, QUERY_HEADS * HEAD_SIZE), 1.0, 6.0, ((0, 16),)),
        "lengths": ragged_sizes(part_splits[6], GROUP_RESPONSES, GROUP_RESPONSES * RESPONSE_LENGTH * 5 // 8, RESPONSE_LENGTH, 1).astype(jnp.int32),
        "doc_mask": touch_ends((jax.random.randint(part_splits[7], (GROUP_RESPONSES, NBLK), 0, 4) < 3).astype(jnp.int32), jax.random.fold_in(part_splits[7], 1), 0, 1),
    }


masked_score = -1.0e30


def reference(queries, response_keys, response_values, document_keys, document_values, grad_out, lengths, doc_mask):
    score_scale = HEAD_SIZE ** -0.5
    slot_index = jnp.arange(RESPONSE_LENGTH, dtype=jnp.int32)
    active_rows = slot_index[None, :] < lengths[:, None]
    query_complete = queries.astype(jnp.float32).reshape(GROUP_RESPONSES, RESPONSE_LENGTH, KEY_HEADS, GROUP_HEADS, HEAD_SIZE)
    gradient_flattened = grad_out.astype(jnp.float32).reshape(GROUP_RESPONSES, RESPONSE_LENGTH, QUERY_HEADS * HEAD_SIZE)
    gradient_full = jnp.where(active_rows[:, :, None], gradient_flattened, jnp.zeros_like(gradient_flattened)).reshape(GROUP_RESPONSES, RESPONSE_LENGTH, KEY_HEADS, GROUP_HEADS, HEAD_SIZE)
    response_own_keys = response_keys.astype(jnp.float32).reshape(GROUP_RESPONSES, RESPONSE_LENGTH, KEY_HEADS, HEAD_SIZE)
    response_own_values = response_values.astype(jnp.float32).reshape(GROUP_RESPONSES, RESPONSE_LENGTH, KEY_HEADS, HEAD_SIZE)
    common_keys = document_keys.astype(jnp.float32).reshape(DOCUMENT_ROWS, KEY_HEADS, HEAD_SIZE)
    common_values = document_values.astype(jnp.float32).reshape(DOCUMENT_ROWS, KEY_HEADS, HEAD_SIZE)
    block_ids = jnp.arange(DOCUMENT_ROWS, dtype=jnp.int32) // SLAB
    causal = slot_index[None, :] <= slot_index[:, None]

    def one_response(carry_grads, inputs):
        key_gradient_total, value_gradient_total = carry_grads
        query_head_rows, grad_heads, keys_own, values_own, mask_row = inputs
        doc_seen = jnp.take(mask_row, block_ids) == 1
        is_seen = jnp.concatenate([jnp.broadcast_to(doc_seen[None, :], (RESPONSE_LENGTH, DOCUMENT_ROWS)), causal], axis=1)
        all_keys = jnp.concatenate([common_keys, keys_own], axis=0)
        all_values = jnp.concatenate([common_values, values_own], axis=0)
        raw_scores = jnp.einsum("tcgd,kcd->tcgk", query_head_rows, all_keys) * score_scale
        raw_scores = jnp.where(is_seen[:, None, None, :], raw_scores, masked_score)
        row_max = jnp.max(raw_scores, axis=-1, keepdims=True)
        exp_terms = jnp.where(is_seen[:, None, None, :], jnp.exp(raw_scores - row_max), 0.0)
        probabilities = exp_terms / jnp.sum(exp_terms, axis=-1, keepdims=True)
        slopes = jnp.einsum("tcgd,kcd->tcgk", grad_heads, all_values)
        row_drift = jnp.sum(probabilities * slopes, axis=-1, keepdims=True)
        mixed_grad = lax.optimization_barrier((probabilities * (slopes - row_drift)).astype(jnp.bfloat16)).astype(jnp.float32)
        prob_low = lax.optimization_barrier(probabilities.astype(jnp.bfloat16)).astype(jnp.float32)
        query_grad = score_scale * jnp.einsum("tcgk,kcd->tcgd", mixed_grad, all_keys)
        key_grad = score_scale * jnp.einsum("tcgk,tcgd->kcd", mixed_grad, query_head_rows)
        value_grad = jnp.einsum("tcgk,tcgd->kcd", prob_low, grad_heads)
        new_carry = (key_gradient_total + key_grad[:DOCUMENT_ROWS], value_gradient_total + value_grad[:DOCUMENT_ROWS])
        return new_carry, (query_grad, key_grad[DOCUMENT_ROWS:], value_grad[DOCUMENT_ROWS:])

    document_zeros = jnp.zeros((DOCUMENT_ROWS, KEY_HEADS, HEAD_SIZE), jnp.float32)
    totals, outputs = lax.scan(one_response, (document_zeros, document_zeros), (query_complete, gradient_full, response_own_keys, response_own_values, doc_mask))
    key_gradient_total, value_gradient_total = totals
    query_grads, response_key_gradient, response_value_gradient = outputs
    return (query_grads.reshape(GROUP_TOKENS, QUERY_HEADS * HEAD_SIZE).astype(jnp.bfloat16),
            key_gradient_total.reshape(DOCUMENT_ROWS, KEY_HEADS * HEAD_SIZE).astype(jnp.bfloat16),
            value_gradient_total.reshape(DOCUMENT_ROWS, KEY_HEADS * HEAD_SIZE).astype(jnp.bfloat16),
            response_key_gradient.reshape(GROUP_TOKENS, KEY_HEADS * HEAD_SIZE).astype(jnp.bfloat16),
            response_value_gradient.reshape(GROUP_TOKENS, KEY_HEADS * HEAD_SIZE).astype(jnp.bfloat16))
```

```python
import jax
import jax.numpy as jnp
from jax import lax
from jax.sharding import PartitionSpec as P

KEY_HEADS = 4
GROUP_HEADS = 5
HEAD_SIZE = 128


masked_score = -1e30


def exchange_bits(size):
    bits = size.bit_length() - 1
    if (1 << bits) != size:
        return None
    return bits


def swap_with(block, axis_name, size, bit):
    pairs = [(index, index ^ (1 << bit)) for index in range(size)]
    return lax.ppermute(block, axis_name, pairs)


def gather_rows(block, axis_name):
    size = lax.axis_size(axis_name)
    bits = exchange_bits(size)
    if bits is None:
        return lax.all_gather(block, axis_name, axis=0, tiled=True)
    me = lax.axis_index(axis_name)
    stacked = block
    for bit in reversed(range(bits)):
        other = swap_with(stacked, axis_name, size, bit)
        mine_low = ((me >> bit) & 1) == 0
        stacked = jnp.where(mine_low, jnp.stack([stacked, other]), jnp.stack([other, stacked]))
    stacked = stacked.reshape((2,) * bits + block.shape)
    stacked = jnp.transpose(stacked, tuple(reversed(range(bits))) + (bits, bits + 1))
    return stacked.reshape((size * block.shape[0],) + block.shape[1:])


def scatter_sum_rows(block, axis_name):
    size = lax.axis_size(axis_name)
    bits = exchange_bits(size)
    if bits is None:
        return lax.psum_scatter(block, axis_name, scatter_dimension=0, tiled=True)
    me = lax.axis_index(axis_name)
    rows = block.shape[0] // size
    parts = block.reshape((2,) * bits + (rows,) + block.shape[1:])
    for bit in range(bits):
        axis = bits - 1 - bit
        mine = (me >> bit) & 1
        keep = lax.dynamic_index_in_dim(parts, mine, axis, keepdims=False)
        send = lax.dynamic_index_in_dim(parts, 1 - mine, axis, keepdims=False)
        parts = keep + swap_with(send, axis_name, size, bit)
    return parts.reshape((rows,) + block.shape[1:])


def per_device(
    queries,
    response_keys,
    response_values,
    document_keys,
    document_values,
    grad_out,
    lengths,
    doc_mask,
):
    token_rows = queries.shape[0]
    responses_here = lengths.shape[0]
    resp_len = token_rows // responses_here
    slab_rows = document_keys.shape[0]
    mask_blocks = doc_mask.shape[1]
    key_value_width = KEY_HEADS * HEAD_SIZE
    score_scale = HEAD_SIZE ** (-0.5)
    positions = jnp.arange(token_rows, dtype=jnp.int32)
    owners = positions // resp_len
    within = positions % resp_len
    active_rows = within < jnp.repeat(lengths, resp_len)
    query_head_rows = queries.reshape(token_rows, KEY_HEADS, GROUP_HEADS, HEAD_SIZE)
    grad_heads = jnp.where(active_rows[:, None], grad_out, jnp.zeros_like(grad_out)).reshape(
        token_rows, KEY_HEADS, GROUP_HEADS, HEAD_SIZE
    )
    response_own_keys = response_keys.reshape(token_rows, KEY_HEADS, HEAD_SIZE)
    response_own_values = response_values.reshape(token_rows, KEY_HEADS, HEAD_SIZE)
    self_visible = (owners[:, None] == owners[None, :]) & (positions[None, :] <= positions[:, None])
    row_masks = jnp.repeat(doc_mask, resp_len, axis=0).astype(jnp.float32)
    collected = gather_rows(jnp.concatenate([document_keys, document_values], axis=1), "resp")
    collected_keys = collected[:, :key_value_width]
    collected_values = collected[:, key_value_width:]
    doc_rows = collected_keys.shape[0]
    block_span = 128
    block_count = doc_rows // block_span
    key_block_list = collected_keys.reshape(block_count, block_span, KEY_HEADS, HEAD_SIZE)
    value_block_list = collected_values.reshape(block_count, block_span, KEY_HEADS, HEAD_SIZE)
    block_index = jnp.arange(block_count, dtype=jnp.int32)

    def visible(first_row, row_count):
        labels = (first_row + jnp.arange(row_count, dtype=jnp.int32)) // slab_rows
        one_hot = (jnp.arange(mask_blocks, dtype=jnp.int32)[:, None] == labels[None, :]).astype(
            jnp.float32
        )
        return jnp.dot(row_masks, one_hot) > 0.5

    def logits(keys_block, is_seen):
        raw_scores = (
            jnp.einsum(
                "tcgd,kcd->tcgk", query_head_rows, keys_block, preferred_element_type=jnp.float32
            )
            * score_scale
        )
        return jnp.where(is_seen[:, None, None, :], raw_scores, masked_score)

    def slopes(values_block):
        return jnp.einsum(
            "tcgd,kcd->tcgk", grad_heads, values_block, preferred_element_type=jnp.float32
        )

    def update_stats(stats_now, keys_block, values_block, is_seen):
        running, denominator, weighted = stats_now
        raw_scores = logits(keys_block, is_seen)
        newest = jnp.maximum(running, jnp.max(raw_scores, axis=-1))
        exp_terms = jnp.where(
            is_seen[:, None, None, :], jnp.exp(raw_scores - newest[..., None]), 0.0
        )
        factor = jnp.exp(running - newest)
        return (
            newest,
            denominator * factor + jnp.sum(exp_terms, axis=-1),
            weighted * factor + jnp.sum(exp_terms * slopes(values_block), axis=-1),
        )

    statistics_shape = (token_rows, KEY_HEADS, GROUP_HEADS)
    first_stats = (
        jnp.full(statistics_shape, masked_score, jnp.float32),
        jnp.zeros(statistics_shape, jnp.float32),
        jnp.zeros(statistics_shape, jnp.float32),
    )
    first_stats = update_stats(first_stats, response_own_keys, response_own_values, self_visible)

    def stats_turn(stats_now, inputs):
        keys_block, values_block, number = inputs
        return (
            update_stats(
                stats_now, keys_block, values_block, visible(number * block_span, block_span)
            ),
            None,
        )

    final_stats, unused = lax.scan(
        stats_turn, first_stats, (key_block_list, value_block_list, block_index)
    )
    running, denominator, weighted = final_stats
    row_drift = weighted / denominator

    def block_grads(keys_block, values_block, is_seen, with_keys):
        raw_scores = logits(keys_block, is_seen)
        probabilities = jnp.where(
            is_seen[:, None, None, :],
            jnp.exp(raw_scores - running[..., None]) / denominator[..., None],
            0.0,
        )
        mixed_grad = (probabilities * (slopes(values_block) - row_drift[..., None])).astype(
            jnp.bfloat16
        )
        query_grad = score_scale * jnp.einsum(
            "tcgk,kcd->tcgd", mixed_grad, keys_block, preferred_element_type=jnp.float32
        )
        if not with_keys:
            return query_grad
        key_grad = score_scale * jnp.einsum(
            "tcgk,tcgd->kcd", mixed_grad, query_head_rows, preferred_element_type=jnp.float32
        )
        value_grad = jnp.einsum(
            "tcgk,tcgd->kcd",
            probabilities.astype(jnp.bfloat16),
            grad_heads,
            preferred_element_type=jnp.float32,
        )
        return (query_grad, key_grad, value_grad)

    response_query, self_key, self_value = block_grads(
        response_own_keys, response_own_values, self_visible, True
    )
    query_initial = jnp.zeros((token_rows, KEY_HEADS, GROUP_HEADS, HEAD_SIZE), jnp.float32)

    def query_turn(query_total, inputs):
        keys_block, values_block, number = inputs
        return (
            query_total
            + block_grads(
                keys_block, values_block, visible(number * block_span, block_span), False
            ),
            None,
        )

    document_query, unused = lax.scan(
        query_turn, query_initial, (key_block_list, value_block_list, block_index)
    )

    def piece_grads(offset, length):
        keys_block = lax.dynamic_slice_in_dim(collected_keys, offset, length, 0).reshape(
            length, KEY_HEADS, HEAD_SIZE
        )
        values_block = lax.dynamic_slice_in_dim(collected_values, offset, length, 0).reshape(
            length, KEY_HEADS, HEAD_SIZE
        )
        unused_query, key_grad, value_grad = block_grads(
            keys_block, values_block, visible(offset, length), True
        )
        return jnp.concatenate(
            [
                key_grad.reshape(length, key_value_width),
                value_grad.reshape(length, key_value_width),
            ],
            axis=1,
        )

    def terms(first_row, row_count):
        if row_count > block_span and row_count % block_span == 0:

            def term_turn(counter, number):
                return (counter, piece_grads(first_row + number * block_span, block_span))

            unused_counter, stacked = lax.scan(
                term_turn,
                jnp.zeros((), jnp.int32),
                jnp.arange(row_count // block_span, dtype=jnp.int32),
            )
            return stacked.reshape(row_count, 2 * key_value_width)
        return piece_grads(first_row, row_count)

    summed = scatter_sum_rows(terms(jnp.int32(0), slab_rows * lax.axis_size("resp")), "resp")
    doc_key_grad = summed[:, :key_value_width]
    doc_value_grad = summed[:, key_value_width:]
    query_gradient = (
        (document_query + response_query)
        .reshape(token_rows, KEY_HEADS * GROUP_HEADS * HEAD_SIZE)
        .astype(jnp.bfloat16)
    )
    return (
        query_gradient,
        doc_key_grad.astype(jnp.bfloat16),
        doc_value_grad.astype(jnp.bfloat16),
        self_key.reshape(token_rows, key_value_width).astype(jnp.bfloat16),
        self_value.reshape(token_rows, key_value_width).astype(jnp.bfloat16),
    )


def solution(mesh):
    return jax.shard_map(
        per_device,
        mesh=mesh,
        in_specs=(
            P(("grp", "resp"), None),
            P(("grp", "resp"), None),
            P(("grp", "resp"), None),
            P(("grp", "resp"), None),
            P(("grp", "resp"), None),
            P(("grp", "resp"), None),
            P(("grp", "resp")),
            P(("grp", "resp"), None),
        ),
        out_specs=(
            P(("grp", "resp"), None),
            P(("grp", "resp"), None),
            P(("grp", "resp"), None),
            P(("grp", "resp"), None),
            P(("grp", "resp"), None),
        ),
        check_vma=False,
    )
```

```python
import jax
import jax.numpy as jnp
from jax import lax
from jax.experimental import pallas as pl
from jax.sharding import PartitionSpec as P

KEY_HEADS = 4
GROUP_HEADS = 5
HEAD_SIZE = 128


masked_score = -1e30


def exchange_bits(size):
    bits = size.bit_length() - 1
    if (1 << bits) != size:
        return None
    return bits


def swap_with(block, axis_name, size, bit):
    pairs = [(index, index ^ (1 << bit)) for index in range(size)]
    return lax.ppermute(block, axis_name, pairs)


def gather_rows(block, axis_name):
    size = lax.axis_size(axis_name)
    bits = exchange_bits(size)
    if bits is None:
        return lax.all_gather(block, axis_name, axis=0, tiled=True)
    me = lax.axis_index(axis_name)
    stacked = block
    for bit in reversed(range(bits)):
        other = swap_with(stacked, axis_name, size, bit)
        mine_low = ((me >> bit) & 1) == 0
        stacked = jnp.where(mine_low, jnp.stack([stacked, other]), jnp.stack([other, stacked]))
    stacked = stacked.reshape((2,) * bits + block.shape)
    stacked = jnp.transpose(stacked, tuple(reversed(range(bits))) + (bits, bits + 1))
    return stacked.reshape((size * block.shape[0],) + block.shape[1:])


def scatter_sum_rows(block, axis_name):
    size = lax.axis_size(axis_name)
    bits = exchange_bits(size)
    if bits is None:
        return lax.psum_scatter(block, axis_name, scatter_dimension=0, tiled=True)
    me = lax.axis_index(axis_name)
    rows = block.shape[0] // size
    parts = block.reshape((2,) * bits + (rows,) + block.shape[1:])
    for bit in range(bits):
        axis = bits - 1 - bit
        mine = (me >> bit) & 1
        keep = lax.dynamic_index_in_dim(parts, mine, axis, keepdims=False)
        send = lax.dynamic_index_in_dim(parts, 1 - mine, axis, keepdims=False)
        parts = keep + swap_with(send, axis_name, size, bit)
    return parts.reshape((rows,) + block.shape[1:])


def contract_rows(left, right):
    return lax.dot_general(
        left, right, (((0,), (0,)), ((), ())), preferred_element_type=jnp.float32
    )


def contract_cols(left, right):
    return lax.dot_general(
        left, right, (((1,), (1,)), ((), ())), preferred_element_type=jnp.float32
    )


def attention_kernel(
    q_ref, do_ref, kv_ref, ks_ref, vs_ref, vis_ref, self_ref, live_ref,
    dq_ref, doc_ref, sk_ref, sv_ref,
):
    token_rows = q_ref.shape[0]
    width = KEY_HEADS * HEAD_SIZE
    score_scale = HEAD_SIZE ** (-0.5)
    doc_seen = jnp.concatenate([vis_ref[...]] * GROUP_HEADS, axis=0) > 0.5
    self_seen = jnp.concatenate([self_ref[...]] * GROUP_HEADS, axis=0) > 0.5
    live = jnp.concatenate([live_ref[...]] * GROUP_HEADS, axis=0) > 0.5
    for c in range(KEY_HEADS):
        kd = kv_ref[:, c * HEAD_SIZE:(c + 1) * HEAD_SIZE]
        vd = kv_ref[:, width + c * HEAD_SIZE:width + (c + 1) * HEAD_SIZE]
        ks = ks_ref[:, c * HEAD_SIZE:(c + 1) * HEAD_SIZE]
        vs = vs_ref[:, c * HEAD_SIZE:(c + 1) * HEAD_SIZE]
        heads = [c * GROUP_HEADS + g for g in range(GROUP_HEADS)]
        q = jnp.concatenate([q_ref[:, h * HEAD_SIZE:(h + 1) * HEAD_SIZE] for h in heads], axis=0)
        do = jnp.concatenate([do_ref[:, h * HEAD_SIZE:(h + 1) * HEAD_SIZE] for h in heads], axis=0)
        do = jnp.where(live, do, jnp.zeros_like(do))
        sd = jnp.where(doc_seen, contract_cols(q, kd) * score_scale, masked_score)
        ss = jnp.where(self_seen, contract_cols(q, ks) * score_scale, masked_score)
        top = jnp.maximum(jnp.max(sd, axis=1, keepdims=True), jnp.max(ss, axis=1, keepdims=True))
        ed = jnp.where(doc_seen, jnp.exp(sd - top), 0.0)
        es = jnp.where(self_seen, jnp.exp(ss - top), 0.0)
        total = jnp.sum(ed, axis=1, keepdims=True) + jnp.sum(es, axis=1, keepdims=True)
        pd = ed / total
        ps = es / total
        gd = contract_cols(do, vd)
        gs = contract_cols(do, vs)
        drift = jnp.sum(pd * gd, axis=1, keepdims=True) + jnp.sum(ps * gs, axis=1, keepdims=True)
        dsd = (pd * (gd - drift)).astype(jnp.bfloat16)
        dss = (ps * (gs - drift)).astype(jnp.bfloat16)
        dq = (
            jnp.dot(dsd, kd, preferred_element_type=jnp.float32)
            + jnp.dot(dss, ks, preferred_element_type=jnp.float32)
        ) * score_scale
        for g, h in enumerate(heads):
            dq_ref[:, h * HEAD_SIZE:(h + 1) * HEAD_SIZE] = dq[
                g * token_rows:(g + 1) * token_rows
            ].astype(dq_ref.dtype)
        doc_ref[:, c * HEAD_SIZE:(c + 1) * HEAD_SIZE] = contract_rows(dsd, q) * score_scale
        doc_ref[:, width + c * HEAD_SIZE:width + (c + 1) * HEAD_SIZE] = contract_rows(
            pd.astype(jnp.bfloat16), do
        )
        sk_ref[:, c * HEAD_SIZE:(c + 1) * HEAD_SIZE] = (
            contract_rows(dss, q) * score_scale
        ).astype(sk_ref.dtype)
        sv_ref[:, c * HEAD_SIZE:(c + 1) * HEAD_SIZE] = contract_rows(
            ps.astype(jnp.bfloat16), do
        ).astype(sv_ref.dtype)


def per_device(
    queries,
    response_keys,
    response_values,
    document_keys,
    document_values,
    grad_out,
    lengths,
    doc_mask,
):
    token_rows = queries.shape[0]
    responses_here = lengths.shape[0]
    resp_len = token_rows // responses_here
    mask_blocks = doc_mask.shape[1]
    key_value_width = KEY_HEADS * HEAD_SIZE
    positions = jnp.arange(token_rows, dtype=jnp.int32)
    owners = positions // resp_len
    within = positions % resp_len
    live = (within < jnp.repeat(lengths, resp_len)).astype(jnp.float32)[:, None]
    self_visible = (
        (owners[:, None] == owners[None, :]) & (positions[None, :] <= positions[:, None])
    ).astype(jnp.float32)
    collected = gather_rows(jnp.concatenate([document_keys, document_values], axis=1), "resp")
    doc_rows = collected.shape[0]
    block_rows = doc_rows // mask_blocks
    row_masks = jnp.repeat(doc_mask, resp_len, axis=0)
    doc_visible = (jnp.repeat(row_masks, block_rows, axis=1) == 1).astype(jnp.float32)
    query_gradient, doc_terms, self_key, self_value = pl.pallas_call(
        attention_kernel,
        out_shape=(
            jax.ShapeDtypeStruct(queries.shape, jnp.bfloat16),
            jax.ShapeDtypeStruct((doc_rows, 2 * key_value_width), jnp.float32),
            jax.ShapeDtypeStruct(response_keys.shape, jnp.bfloat16),
            jax.ShapeDtypeStruct(response_values.shape, jnp.bfloat16),
        ),
    )(
        queries,
        grad_out,
        collected,
        response_keys,
        response_values,
        doc_visible,
        self_visible,
        live,
    )
    summed = scatter_sum_rows(doc_terms, "resp")
    return (
        query_gradient,
        summed[:, :key_value_width].astype(jnp.bfloat16),
        summed[:, key_value_width:].astype(jnp.bfloat16),
        self_key,
        self_value,
    )


def solution(mesh):
    return jax.shard_map(
        per_device,
        mesh=mesh,
        in_specs=(
            P(("grp", "resp"), None),
            P(("grp", "resp"), None),
            P(("grp", "resp"), None),
            P(("grp", "resp"), None),
            P(("grp", "resp"), None),
            P(("grp", "resp"), None),
            P(("grp", "resp")),
            P(("grp", "resp"), None),
        ),
        out_specs=(
            P(("grp", "resp"), None),
            P(("grp", "resp"), None),
            P(("grp", "resp"), None),
            P(("grp", "resp"), None),
            P(("grp", "resp"), None),
        ),
        check_vma=False,
    )
```

```python
import jax
import numpy as np
import jax.numpy as jnp
from jax import lax
from jax.experimental import pallas as pl
from jax.sharding import PartitionSpec as P

KEY_HEADS = 4
GROUP_HEADS = 5
HEAD_SIZE = 128


masked_score = -1e30


def exchange_bits(size):
    bits = size.bit_length() - 1
    if (1 << bits) != size:
        return None
    return bits


def swap_with(block, axis_name, size, bit):
    pairs = [(index, index ^ (1 << bit)) for index in range(size)]
    return lax.ppermute(block, axis_name, pairs)


def reversed_order(size):
    bits = exchange_bits(size)
    if not bits:
        return list(range(size))
    return [int(format(spot, "0%db" % bits)[::-1], 2) for spot in range(size)]


def gather_rows(block, axis_name):
    size = lax.axis_size(axis_name)
    bits = exchange_bits(size)
    if bits is None:
        return lax.all_gather(block, axis_name, axis=0, tiled=True)
    me = lax.axis_index(axis_name)
    stacked = block
    for bit in reversed(range(bits)):
        other = swap_with(stacked, axis_name, size, bit)
        mine_low = ((me >> bit) & 1) == 0
        stacked = jnp.where(mine_low, jnp.stack([stacked, other]), jnp.stack([other, stacked]))
    return stacked.reshape((size * block.shape[0],) + block.shape[1:])


def scatter_sum_rows(block, axis_name):
    size = lax.axis_size(axis_name)
    bits = exchange_bits(size)
    if not bits:
        return lax.psum_scatter(block, axis_name, scatter_dimension=0, tiled=True)
    me = lax.axis_index(axis_name)
    parts = block.reshape((2, block.shape[0] // 2) + block.shape[1:])
    for bit in range(bits):
        mine = (me >> bit) & 1
        keep = lax.dynamic_index_in_dim(parts, mine, 0, keepdims=False)
        send = lax.dynamic_index_in_dim(parts, 1 - mine, 0, keepdims=False)
        parts = keep + swap_with(send, axis_name, size, bit)
        if bit + 1 < bits:
            parts = parts.reshape((2, parts.shape[0] // 2) + parts.shape[1:])
    return parts


def contract_rows(left, right):
    return lax.dot_general(
        left, right, (((0,), (0,)), ((), ())), preferred_element_type=jnp.float32
    )


def contract_cols(left, right):
    return lax.dot_general(
        left, right, (((1,), (1,)), ((), ())), preferred_element_type=jnp.float32
    )


def attention_kernel(
    q_ref, do_ref, kv_ref, ks_ref, vs_ref, vis_ref, self_ref, live_ref,
    dq_ref, doc_ref, sk_ref, sv_ref,
):
    token_rows = q_ref.shape[0]
    width = KEY_HEADS * HEAD_SIZE
    score_scale = HEAD_SIZE ** (-0.5)
    doc_seen = jnp.concatenate([vis_ref[...]] * GROUP_HEADS, axis=0) > 0.5
    self_seen = jnp.concatenate([self_ref[...]] * GROUP_HEADS, axis=0) > 0.5
    live = jnp.concatenate([live_ref[...]] * GROUP_HEADS, axis=0) > 0.5
    for c in range(KEY_HEADS):
        kd = kv_ref[:, c * HEAD_SIZE:(c + 1) * HEAD_SIZE]
        vd = kv_ref[:, width + c * HEAD_SIZE:width + (c + 1) * HEAD_SIZE]
        ks = ks_ref[:, c * HEAD_SIZE:(c + 1) * HEAD_SIZE]
        vs = vs_ref[:, c * HEAD_SIZE:(c + 1) * HEAD_SIZE]
        heads = [c * GROUP_HEADS + g for g in range(GROUP_HEADS)]
        q = jnp.concatenate([q_ref[:, h * HEAD_SIZE:(h + 1) * HEAD_SIZE] for h in heads], axis=0)
        do = jnp.concatenate([do_ref[:, h * HEAD_SIZE:(h + 1) * HEAD_SIZE] for h in heads], axis=0)
        do = jnp.where(live, do, jnp.zeros_like(do))
        sd = jnp.where(doc_seen, contract_cols(q, kd) * score_scale, masked_score)
        ss = jnp.where(self_seen, contract_cols(q, ks) * score_scale, masked_score)
        top = jnp.maximum(jnp.max(sd, axis=1, keepdims=True), jnp.max(ss, axis=1, keepdims=True))
        ed = jnp.where(doc_seen, jnp.exp(sd - top), 0.0)
        es = jnp.where(self_seen, jnp.exp(ss - top), 0.0)
        total = jnp.sum(ed, axis=1, keepdims=True) + jnp.sum(es, axis=1, keepdims=True)
        pd = ed / total
        ps = es / total
        gd = contract_cols(do, vd)
        gs = contract_cols(do, vs)
        drift = jnp.sum(pd * gd, axis=1, keepdims=True) + jnp.sum(ps * gs, axis=1, keepdims=True)
        dsd = (pd * (gd - drift)).astype(jnp.bfloat16)
        dss = (ps * (gs - drift)).astype(jnp.bfloat16)
        dq = (
            jnp.dot(dsd, kd, preferred_element_type=jnp.float32)
            + jnp.dot(dss, ks, preferred_element_type=jnp.float32)
        ) * score_scale
        for g, h in enumerate(heads):
            dq_ref[:, h * HEAD_SIZE:(h + 1) * HEAD_SIZE] = dq[
                g * token_rows:(g + 1) * token_rows
            ].astype(dq_ref.dtype)
        doc_ref[:, c * HEAD_SIZE:(c + 1) * HEAD_SIZE] = contract_rows(dsd, q) * score_scale
        doc_ref[:, width + c * HEAD_SIZE:width + (c + 1) * HEAD_SIZE] = contract_rows(
            pd.astype(jnp.bfloat16), do
        )
        sk_ref[:, c * HEAD_SIZE:(c + 1) * HEAD_SIZE] = (
            contract_rows(dss, q) * score_scale
        ).astype(sk_ref.dtype)
        sv_ref[:, c * HEAD_SIZE:(c + 1) * HEAD_SIZE] = contract_rows(
            ps.astype(jnp.bfloat16), do
        ).astype(sv_ref.dtype)


def per_device(
    queries,
    response_keys,
    response_values,
    document_keys,
    document_values,
    grad_out,
    lengths,
    doc_mask,
):
    token_rows = queries.shape[0]
    responses_here = lengths.shape[0]
    resp_len = token_rows // responses_here
    mask_blocks = doc_mask.shape[1]
    key_value_width = KEY_HEADS * HEAD_SIZE
    positions = jnp.arange(token_rows, dtype=jnp.int32)
    owners = positions // resp_len
    within = positions % resp_len
    live = (within < jnp.repeat(lengths, resp_len)).astype(jnp.float32)[:, None]
    self_visible = (
        (owners[:, None] == owners[None, :]) & (positions[None, :] <= positions[:, None])
    ).astype(jnp.float32)
    collected = gather_rows(jnp.concatenate([document_keys, document_values], axis=1), "resp")
    doc_rows = collected.shape[0]
    block_rows = doc_rows // mask_blocks
    slab_rows = document_keys.shape[0]
    holders = np.repeat(np.array(reversed_order(lax.axis_size("resp"))), slab_rows)
    global_rows = holders * slab_rows + np.tile(np.arange(slab_rows), lax.axis_size("resp"))
    row_masks = jnp.repeat(doc_mask, resp_len, axis=0)
    doc_visible = (row_masks[:, global_rows // block_rows] == 1).astype(jnp.float32)
    query_gradient, doc_terms, self_key, self_value = pl.pallas_call(
        attention_kernel,
        out_shape=(
            jax.ShapeDtypeStruct(queries.shape, jnp.bfloat16),
            jax.ShapeDtypeStruct((doc_rows, 2 * key_value_width), jnp.float32),
            jax.ShapeDtypeStruct(response_keys.shape, jnp.bfloat16),
            jax.ShapeDtypeStruct(response_values.shape, jnp.bfloat16),
        ),
    )(
        queries,
        grad_out,
        collected,
        response_keys,
        response_values,
        doc_visible,
        self_visible,
        live,
    )
    summed = scatter_sum_rows(doc_terms, "resp")
    return (
        query_gradient,
        summed[:, :key_value_width].astype(jnp.bfloat16),
        summed[:, key_value_width:].astype(jnp.bfloat16),
        self_key,
        self_value,
    )


def solution(mesh):
    return jax.shard_map(
        per_device,
        mesh=mesh,
        in_specs=(
            P(("grp", "resp"), None),
            P(("grp", "resp"), None),
            P(("grp", "resp"), None),
            P(("grp", "resp"), None),
            P(("grp", "resp"), None),
            P(("grp", "resp"), None),
            P(("grp", "resp")),
            P(("grp", "resp"), None),
        ),
        out_specs=(
            P(("grp", "resp"), None),
            P(("grp", "resp"), None),
            P(("grp", "resp"), None),
            P(("grp", "resp"), None),
            P(("grp", "resp"), None),
        ),
        check_vma=False,
    )
```

```python
import jax
import numpy as np
import jax.numpy as jnp
from jax import lax
from jax.experimental import pallas as pl
from jax.sharding import PartitionSpec as P

KEY_HEADS = 4
GROUP_HEADS = 5
HEAD_SIZE = 128


masked_score = -1e30


def exchange_bits(size):
    bits = size.bit_length() - 1
    if (1 << bits) != size:
        return None
    return bits


def swap_with(block, axis_name, size, bit):
    pairs = [(index, index ^ (1 << bit)) for index in range(size)]
    return lax.ppermute(block, axis_name, pairs)


def exchange_pattern(size):
    bits = exchange_bits(size)
    return [int(format(spot, "0%db" % bits)[::-1], 2) for spot in range(size)]


def gather_rows(blocks, axis_name):
    size = lax.axis_size(axis_name)
    bits = exchange_bits(size)
    halves = None
    for bit in reversed(range(bits)):
        if halves is not None:
            blocks = jnp.concatenate(halves)
        halves = (blocks, swap_with(blocks, axis_name, size, bit))
    return halves


def scatter_sum_rows(keep, send, axis_name):
    size = lax.axis_size(axis_name)
    bits = exchange_bits(size)
    for bit in range(bits):
        if bit > 0:
            split = keep.shape[0] // 2
            keep, send = keep[:split], keep[split:]
        keep = keep + swap_with(send, axis_name, size, bit)
    return keep


def contract_rows(left, right):
    return lax.dot_general(
        left, right, (((0,), (0,)), ((), ())), preferred_element_type=jnp.float32
    )


def contract_cols(left, right):
    return lax.dot_general(
        left, right, (((1,), (1,)), ((), ())), preferred_element_type=jnp.float32
    )


def attention_kernel(
    q_ref, do_ref, kva_ref, kvb_ref, ks_ref, vs_ref, vis_ref, self_ref, live_ref,
    dq_ref, keep_ref, send_ref, sk_ref, sv_ref,
):
    token_rows = q_ref.shape[0]
    width = KEY_HEADS * HEAD_SIZE
    half = kva_ref.shape[0]
    score_scale = HEAD_SIZE ** (-0.5)
    doc_seen = jnp.concatenate([vis_ref[...]] * GROUP_HEADS, axis=0) > 0.5
    self_seen = jnp.concatenate([self_ref[...]] * GROUP_HEADS, axis=0) > 0.5
    live = jnp.concatenate([live_ref[...]] * GROUP_HEADS, axis=0) > 0.5
    for c in range(KEY_HEADS):
        columns = slice(c * HEAD_SIZE, (c + 1) * HEAD_SIZE)
        value_columns = slice(width + c * HEAD_SIZE, width + (c + 1) * HEAD_SIZE)
        kd = jnp.concatenate([kva_ref[:, columns], kvb_ref[:, columns]], axis=0)
        vd = jnp.concatenate([kva_ref[:, value_columns], kvb_ref[:, value_columns]], axis=0)
        ks = ks_ref[:, c * HEAD_SIZE:(c + 1) * HEAD_SIZE]
        vs = vs_ref[:, c * HEAD_SIZE:(c + 1) * HEAD_SIZE]
        heads = [c * GROUP_HEADS + g for g in range(GROUP_HEADS)]
        q = jnp.concatenate([q_ref[:, h * HEAD_SIZE:(h + 1) * HEAD_SIZE] for h in heads], axis=0)
        do = jnp.concatenate([do_ref[:, h * HEAD_SIZE:(h + 1) * HEAD_SIZE] for h in heads], axis=0)
        do = jnp.where(live, do, jnp.zeros_like(do))
        sd = jnp.where(doc_seen, contract_cols(q, kd) * score_scale, masked_score)
        ss = jnp.where(self_seen, contract_cols(q, ks) * score_scale, masked_score)
        top = jnp.maximum(jnp.max(sd, axis=1, keepdims=True), jnp.max(ss, axis=1, keepdims=True))
        ed = jnp.where(doc_seen, jnp.exp(sd - top), 0.0)
        es = jnp.where(self_seen, jnp.exp(ss - top), 0.0)
        total = jnp.sum(ed, axis=1, keepdims=True) + jnp.sum(es, axis=1, keepdims=True)
        pd = ed / total
        ps = es / total
        gd = contract_cols(do, vd)
        gs = contract_cols(do, vs)
        drift = jnp.sum(pd * gd, axis=1, keepdims=True) + jnp.sum(ps * gs, axis=1, keepdims=True)
        dsd = (pd * (gd - drift)).astype(jnp.bfloat16)
        dss = (ps * (gs - drift)).astype(jnp.bfloat16)
        dq = (
            jnp.dot(dsd, kd, preferred_element_type=jnp.float32)
            + jnp.dot(dss, ks, preferred_element_type=jnp.float32)
        ) * score_scale
        for g, h in enumerate(heads):
            dq_ref[:, h * HEAD_SIZE:(h + 1) * HEAD_SIZE] = dq[
                g * token_rows:(g + 1) * token_rows
            ].astype(dq_ref.dtype)
        doc_key = contract_rows(dsd, q) * score_scale
        doc_value = contract_rows(pd.astype(jnp.bfloat16), do)
        keep_ref[:, columns] = doc_key[:half]
        send_ref[:, columns] = doc_key[half:]
        keep_ref[:, value_columns] = doc_value[:half]
        send_ref[:, value_columns] = doc_value[half:]
        sk_ref[:, c * HEAD_SIZE:(c + 1) * HEAD_SIZE] = (
            contract_rows(dss, q) * score_scale
        ).astype(sk_ref.dtype)
        sv_ref[:, c * HEAD_SIZE:(c + 1) * HEAD_SIZE] = contract_rows(
            ps.astype(jnp.bfloat16), do
        ).astype(sv_ref.dtype)


def per_device(
    queries,
    response_keys,
    response_values,
    document_keys,
    document_values,
    grad_out,
    lengths,
    doc_mask,
):
    token_rows = queries.shape[0]
    responses_here = lengths.shape[0]
    resp_len = token_rows // responses_here
    mask_blocks = doc_mask.shape[1]
    key_value_width = KEY_HEADS * HEAD_SIZE
    positions = jnp.arange(token_rows, dtype=jnp.int32)
    owners = positions // resp_len
    within = positions % resp_len
    live = (within < jnp.repeat(lengths, resp_len)).astype(jnp.float32)[:, None]
    self_visible = (
        (owners[:, None] == owners[None, :]) & (positions[None, :] <= positions[:, None])
    ).astype(jnp.float32)
    size = lax.axis_size("resp")
    doc_mine, doc_other = gather_rows(
        jnp.concatenate([document_keys, document_values], axis=1), "resp"
    )
    slab_rows = document_keys.shape[0]
    doc_rows = size * slab_rows
    half_rows = doc_rows // 2
    block_rows = doc_rows // mask_blocks
    holders = jnp.bitwise_xor(
        lax.axis_index("resp"), jnp.asarray(np.repeat(exchange_pattern(size), slab_rows), jnp.int32)
    )
    global_rows = holders * slab_rows + jnp.asarray(np.tile(np.arange(slab_rows), size), jnp.int32)
    row_masks = jnp.repeat(doc_mask, resp_len, axis=0)
    doc_visible = (jnp.take(row_masks, global_rows // block_rows, axis=1) == 1).astype(jnp.float32)
    query_gradient, doc_keep, doc_send, self_key, self_value = pl.pallas_call(
        attention_kernel,
        out_shape=(
            jax.ShapeDtypeStruct(queries.shape, jnp.bfloat16),
            jax.ShapeDtypeStruct((half_rows, 2 * key_value_width), jnp.float32),
            jax.ShapeDtypeStruct((half_rows, 2 * key_value_width), jnp.float32),
            jax.ShapeDtypeStruct(response_keys.shape, jnp.bfloat16),
            jax.ShapeDtypeStruct(response_values.shape, jnp.bfloat16),
        ),
    )(
        queries,
        grad_out,
        doc_mine,
        doc_other,
        response_keys,
        response_values,
        doc_visible,
        self_visible,
        live,
    )
    summed = scatter_sum_rows(doc_keep, doc_send, "resp")
    return (
        query_gradient,
        summed[:, :key_value_width].astype(jnp.bfloat16),
        summed[:, key_value_width:].astype(jnp.bfloat16),
        self_key,
        self_value,
    )


def solution(mesh):
    return jax.shard_map(
        per_device,
        mesh=mesh,
        in_specs=(
            P(("grp", "resp"), None),
            P(("grp", "resp"), None),
            P(("grp", "resp"), None),
            P(("grp", "resp"), None),
            P(("grp", "resp"), None),
            P(("grp", "resp"), None),
            P(("grp", "resp")),
            P(("grp", "resp"), None),
        ),
        out_specs=(
            P(("grp", "resp"), None),
            P(("grp", "resp"), None),
            P(("grp", "resp"), None),
            P(("grp", "resp"), None),
            P(("grp", "resp"), None),
        ),
        check_vma=False,
    )
```

```python
import jax
import numpy as np
import jax.numpy as jnp
from jax import lax
from jax.experimental import pallas as pl
from jax.sharding import PartitionSpec as P

KEY_HEADS = 4
GROUP_HEADS = 5
HEAD_SIZE = 128


masked_score = -1e30


def exchange_bits(size):
    bits = size.bit_length() - 1
    if (1 << bits) != size:
        return None
    return bits


def swap_with(block, axis_name, size, bit):
    pairs = [(index, index ^ (1 << bit)) for index in range(size)]
    return lax.ppermute(block, axis_name, pairs)


def exchange_pattern(size):
    bits = exchange_bits(size)
    return [int(format(spot, "0%db" % bits)[::-1], 2) for spot in range(size)]


def gather_rows(blocks, axis_name):
    size = lax.axis_size(axis_name)
    bits = exchange_bits(size)
    halves = None
    for bit in reversed(range(bits)):
        if halves is not None:
            blocks = jnp.concatenate(halves)
        halves = (blocks, swap_with(blocks, axis_name, size, bit))
    return halves


def scatter_sum_rows(keep, send, axis_name):
    size = lax.axis_size(axis_name)
    bits = exchange_bits(size)
    for bit in range(bits):
        if bit > 0:
            split = keep.shape[0] // 2
            keep, send = keep[:split], keep[split:]
        keep = keep + swap_with(send, axis_name, size, bit)
    return keep


def contract_rows(left, right):
    return lax.dot_general(
        left, right, (((0,), (0,)), ((), ())), preferred_element_type=jnp.float32
    )


def contract_cols(left, right):
    return lax.dot_general(
        left, right, (((1,), (1,)), ((), ())), preferred_element_type=jnp.float32
    )


def stacked_heads(ref, c):
    return jnp.concatenate(
        [
            ref[:, h * HEAD_SIZE:(h + 1) * HEAD_SIZE]
            for h in range(c * GROUP_HEADS, (c + 1) * GROUP_HEADS)
        ],
        axis=0,
    )


def live_rows(owner_ref, within_ref, lengths_ref):
    owner = owner_ref[...]
    limit = jnp.zeros_like(owner)
    for response in range(lengths_ref.shape[1]):
        limit = jnp.where(owner == response, lengths_ref[:, response:response + 1], limit)
    return jnp.concatenate([within_ref[...] < limit] * GROUP_HEADS, axis=0)


def head_columns(c, offset=0):
    return slice(offset + c * HEAD_SIZE, offset + (c + 1) * HEAD_SIZE)


def self_stats_kernel(
    q_ref, do_ref, ks_ref, vs_ref, self_ref, owner_ref, within_ref, lengths_ref, stats_ref
):
    score_scale = HEAD_SIZE ** (-0.5)
    self_seen = jnp.concatenate([self_ref[...]] * GROUP_HEADS, axis=0) > 0.5
    live = live_rows(owner_ref, within_ref, lengths_ref)
    stats_ref[...] = jnp.zeros_like(stats_ref)
    for c in range(KEY_HEADS):
        q = stacked_heads(q_ref, c)
        do = stacked_heads(do_ref, c)
        do = jnp.where(live, do, jnp.zeros_like(do))
        ss = jnp.where(self_seen, contract_cols(q, ks_ref[:, head_columns(c)]) * score_scale, masked_score)
        top = jnp.max(ss, axis=1, keepdims=True)
        es = jnp.where(self_seen, jnp.exp(ss - top), 0.0)
        gs = contract_cols(do, vs_ref[:, head_columns(c)])
        stats_ref[:, c:c + 1] = top
        stats_ref[:, KEY_HEADS + c:KEY_HEADS + c + 1] = jnp.sum(es, axis=1, keepdims=True)
        stats_ref[:, 2 * KEY_HEADS + c:2 * KEY_HEADS + c + 1] = jnp.sum(es * gs, axis=1, keepdims=True)


def document_kernel(
    q_ref, do_ref, kva_ref, kvb_ref, vis_ref, self_stats_ref, owner_ref, within_ref, lengths_ref,
    keep_ref, send_ref, stats_ref, dsd_ref,
):
    width = KEY_HEADS * HEAD_SIZE
    half = kva_ref.shape[0]
    score_scale = HEAD_SIZE ** (-0.5)
    doc_seen = jnp.concatenate([vis_ref[...]] * GROUP_HEADS, axis=0) > 0.5
    live = live_rows(owner_ref, within_ref, lengths_ref)
    stats_ref[...] = jnp.zeros_like(stats_ref)
    for c in range(KEY_HEADS):
        kd = jnp.concatenate([kva_ref[:, head_columns(c)], kvb_ref[:, head_columns(c)]], axis=0)
        vd = jnp.concatenate(
            [kva_ref[:, head_columns(c, width)], kvb_ref[:, head_columns(c, width)]], axis=0
        )
        q = stacked_heads(q_ref, c)
        do = stacked_heads(do_ref, c)
        do = jnp.where(live, do, jnp.zeros_like(do))
        self_top = self_stats_ref[:, c:c + 1]
        self_total = self_stats_ref[:, KEY_HEADS + c:KEY_HEADS + c + 1]
        self_weighted = self_stats_ref[:, 2 * KEY_HEADS + c:2 * KEY_HEADS + c + 1]
        sd = jnp.where(doc_seen, contract_cols(q, kd) * score_scale, masked_score)
        top = jnp.maximum(jnp.max(sd, axis=1, keepdims=True), self_top)
        ed = jnp.where(doc_seen, jnp.exp(sd - top), 0.0)
        factor = jnp.exp(self_top - top)
        gd = contract_cols(do, vd)
        total = jnp.sum(ed, axis=1, keepdims=True) + self_total * factor
        drift = (jnp.sum(ed * gd, axis=1, keepdims=True) + self_weighted * factor) / total
        pd = ed / total
        dsd = (pd * (gd - drift)).astype(jnp.bfloat16)
        dsd_ref[c] = dsd
        stats_ref[:, c:c + 1] = top
        stats_ref[:, KEY_HEADS + c:KEY_HEADS + c + 1] = total
        stats_ref[:, 2 * KEY_HEADS + c:2 * KEY_HEADS + c + 1] = drift
        doc_key = contract_rows(dsd, q) * score_scale
        doc_value = contract_rows(pd.astype(jnp.bfloat16), do)
        keep_ref[:, head_columns(c)] = doc_key[:half]
        send_ref[:, head_columns(c)] = doc_key[half:]
        keep_ref[:, head_columns(c, width)] = doc_value[:half]
        send_ref[:, head_columns(c, width)] = doc_value[half:]


def response_kernel(
    q_ref, do_ref, kva_ref, kvb_ref, ks_ref, vs_ref, stats_ref, dsd_ref, self_ref,
    owner_ref, within_ref, lengths_ref,
    dq_ref, sk_ref, sv_ref,
):
    token_rows = q_ref.shape[0]
    score_scale = HEAD_SIZE ** (-0.5)
    self_seen = jnp.concatenate([self_ref[...]] * GROUP_HEADS, axis=0) > 0.5
    live = live_rows(owner_ref, within_ref, lengths_ref)
    for c in range(KEY_HEADS):
        kd = jnp.concatenate([kva_ref[:, head_columns(c)], kvb_ref[:, head_columns(c)]], axis=0)
        ks = ks_ref[:, head_columns(c)]
        q = stacked_heads(q_ref, c)
        do = stacked_heads(do_ref, c)
        do = jnp.where(live, do, jnp.zeros_like(do))
        top = stats_ref[:, c:c + 1]
        total = stats_ref[:, KEY_HEADS + c:KEY_HEADS + c + 1]
        drift = stats_ref[:, 2 * KEY_HEADS + c:2 * KEY_HEADS + c + 1]
        ss = jnp.where(self_seen, contract_cols(q, ks) * score_scale, masked_score)
        ps = jnp.where(self_seen, jnp.exp(ss - top), 0.0) / total
        gs = contract_cols(do, vs_ref[:, head_columns(c)])
        dss = (ps * (gs - drift)).astype(jnp.bfloat16)
        dq = (
            jnp.dot(dsd_ref[c], kd, preferred_element_type=jnp.float32)
            + jnp.dot(dss, ks, preferred_element_type=jnp.float32)
        ) * score_scale
        for g in range(GROUP_HEADS):
            h = c * GROUP_HEADS + g
            dq_ref[:, h * HEAD_SIZE:(h + 1) * HEAD_SIZE] = dq[
                g * token_rows:(g + 1) * token_rows
            ].astype(dq_ref.dtype)
        sk_ref[:, head_columns(c)] = (contract_rows(dss, q) * score_scale).astype(sk_ref.dtype)
        sv_ref[:, head_columns(c)] = contract_rows(ps.astype(jnp.bfloat16), do).astype(
            sv_ref.dtype
        )


def per_device(
    queries,
    response_keys,
    response_values,
    document_keys,
    document_values,
    grad_out,
    lengths,
    doc_mask,
):
    token_rows = queries.shape[0]
    responses_here = lengths.shape[0]
    resp_len = token_rows // responses_here
    mask_blocks = doc_mask.shape[1]
    key_value_width = KEY_HEADS * HEAD_SIZE
    stacked_rows = GROUP_HEADS * token_rows
    positions = np.arange(token_rows)
    owners = positions // resp_len
    owner_column = jnp.asarray(owners[:, None], jnp.int32)
    within_column = jnp.asarray((positions % resp_len)[:, None], jnp.int32)
    self_visible = jnp.asarray(
        (owners[:, None] == owners[None, :]) & (positions[None, :] <= positions[:, None]),
        jnp.float32,
    )
    lengths_row = lengths.reshape(1, responses_here)
    self_stats = pl.pallas_call(
        self_stats_kernel,
        out_shape=jax.ShapeDtypeStruct((stacked_rows, 128), jnp.float32),
    )(
        queries, grad_out, response_keys, response_values, self_visible,
        owner_column, within_column, lengths_row,
    )
    size = lax.axis_size("resp")
    doc_mine, doc_other = gather_rows(
        jnp.concatenate([document_keys, document_values], axis=1), "resp"
    )
    slab_rows = document_keys.shape[0]
    doc_rows = size * slab_rows
    half_rows = doc_rows // 2
    block_rows = doc_rows // mask_blocks
    holders = jnp.bitwise_xor(
        lax.axis_index("resp"), jnp.asarray(np.repeat(exchange_pattern(size), slab_rows), jnp.int32)
    )
    global_rows = holders * slab_rows + jnp.asarray(np.tile(np.arange(slab_rows), size), jnp.int32)
    row_masks = jnp.repeat(doc_mask, resp_len, axis=0)
    doc_visible = (jnp.take(row_masks, global_rows // block_rows, axis=1) == 1).astype(jnp.float32)
    doc_keep, doc_send, row_stats, doc_dscore = pl.pallas_call(
        document_kernel,
        out_shape=(
            jax.ShapeDtypeStruct((half_rows, 2 * key_value_width), jnp.float32),
            jax.ShapeDtypeStruct((half_rows, 2 * key_value_width), jnp.float32),
            jax.ShapeDtypeStruct((stacked_rows, 128), jnp.float32),
            jax.ShapeDtypeStruct((KEY_HEADS, stacked_rows, doc_rows), jnp.bfloat16),
        ),
    )(
        queries, grad_out, doc_mine, doc_other, doc_visible, self_stats,
        owner_column, within_column, lengths_row,
    )
    summed = scatter_sum_rows(doc_keep, doc_send, "resp")
    query_gradient, self_key, self_value = pl.pallas_call(
        response_kernel,
        out_shape=(
            jax.ShapeDtypeStruct(queries.shape, jnp.bfloat16),
            jax.ShapeDtypeStruct(response_keys.shape, jnp.bfloat16),
            jax.ShapeDtypeStruct(response_values.shape, jnp.bfloat16),
        ),
    )(
        queries, grad_out, doc_mine, doc_other, response_keys, response_values,
        row_stats, doc_dscore, self_visible, owner_column, within_column, lengths_row,
    )
    return (
        query_gradient,
        summed[:, :key_value_width].astype(jnp.bfloat16),
        summed[:, key_value_width:].astype(jnp.bfloat16),
        self_key,
        self_value,
    )


def solution(mesh):
    return jax.shard_map(
        per_device,
        mesh=mesh,
        in_specs=(
            P(("grp", "resp"), None),
            P(("grp", "resp"), None),
            P(("grp", "resp"), None),
            P(("grp", "resp"), None),
            P(("grp", "resp"), None),
            P(("grp", "resp"), None),
            P(("grp", "resp")),
            P(("grp", "resp"), None),
        ),
        out_specs=(
            P(("grp", "resp"), None),
            P(("grp", "resp"), None),
            P(("grp", "resp"), None),
            P(("grp", "resp"), None),
            P(("grp", "resp"), None),
        ),
        check_vma=False,
    )
```

```python
import jax
import numpy as np
import jax.numpy as jnp
from jax import lax
from jax.experimental import pallas as pl
from jax.sharding import PartitionSpec as P

KEY_HEADS = 4
GROUP_HEADS = 5
HEAD_SIZE = 128


masked_score = -1e30


def exchange_bits(size):
    bits = size.bit_length() - 1
    if (1 << bits) != size:
        return None
    return bits


def swap_with(block, axis_name, size, bit):
    pairs = [(index, index ^ (1 << bit)) for index in range(size)]
    return lax.ppermute(block, axis_name, pairs)


def exchange_pattern(size):
    bits = exchange_bits(size)
    return [int(format(spot, "0%db" % bits)[::-1], 2) for spot in range(size)]


def gather_rows(blocks, axis_name):
    size = lax.axis_size(axis_name)
    bits = exchange_bits(size)
    halves = None
    for bit in reversed(range(bits)):
        if halves is not None:
            blocks = jnp.concatenate(halves)
        halves = (blocks, swap_with(blocks, axis_name, size, bit))
    return halves


def scatter_sum_rows(keep, send, axis_name):
    size = lax.axis_size(axis_name)
    bits = exchange_bits(size)
    for bit in range(bits):
        if bit > 0:
            split = keep.shape[0] // 2
            keep, send = keep[:split], keep[split:]
        keep = keep + swap_with(send, axis_name, size, bit)
    return keep


def contract_rows(left, right):
    return lax.dot_general(
        left, right, (((0,), (0,)), ((), ())), preferred_element_type=jnp.float32
    )


def contract_cols(left, right):
    return lax.dot_general(
        left, right, (((1,), (1,)), ((), ())), preferred_element_type=jnp.float32
    )


def stacked_heads(ref, c):
    return jnp.concatenate(
        [
            ref[:, h * HEAD_SIZE:(h + 1) * HEAD_SIZE]
            for h in range(c * GROUP_HEADS, (c + 1) * GROUP_HEADS)
        ],
        axis=0,
    )


def attention_kernel(
    q_ref, do_ref, kva_ref, kvb_ref, ks_ref, vs_ref, vis_ref, self_ref, live_ref,
    dq_ref, keep_ref, send_ref, sk_ref, sv_ref,
):
    token_rows = q_ref.shape[0]
    width = KEY_HEADS * HEAD_SIZE
    half = kva_ref.shape[0]
    score_scale = HEAD_SIZE ** (-0.5)
    doc_seen = jnp.concatenate([vis_ref[...]] * GROUP_HEADS, axis=1) > 0.5
    self_seen = jnp.concatenate([self_ref[...]] * GROUP_HEADS, axis=1) > 0.5
    live = jnp.concatenate([live_ref[...]] * GROUP_HEADS, axis=1)
    for c in range(KEY_HEADS):
        columns = slice(c * HEAD_SIZE, (c + 1) * HEAD_SIZE)
        value_columns = slice(width + c * HEAD_SIZE, width + (c + 1) * HEAD_SIZE)
        kd = jnp.concatenate([kva_ref[:, columns], kvb_ref[:, columns]], axis=0)
        vd = jnp.concatenate([kva_ref[:, value_columns], kvb_ref[:, value_columns]], axis=0)
        ks = ks_ref[:, columns]
        vs = vs_ref[:, columns]
        q = stacked_heads(q_ref, c)
        do = stacked_heads(do_ref, c)
        sd = jnp.where(doc_seen, contract_cols(kd, q) * score_scale, masked_score)
        ss = jnp.where(self_seen, contract_cols(ks, q) * score_scale, masked_score)
        top = jnp.maximum(jnp.max(sd, axis=0, keepdims=True), jnp.max(ss, axis=0, keepdims=True))
        ed = jnp.where(doc_seen, jnp.exp(sd - top), 0.0)
        es = jnp.where(self_seen, jnp.exp(ss - top), 0.0)
        total = jnp.sum(ed, axis=0, keepdims=True) + jnp.sum(es, axis=0, keepdims=True)
        pd = ed / total
        ps = es / total
        gd = contract_cols(vd, do) * live
        gs = contract_cols(vs, do) * live
        drift = jnp.sum(pd * gd, axis=0, keepdims=True) + jnp.sum(ps * gs, axis=0, keepdims=True)
        dsd = (pd * (gd - drift)).astype(jnp.bfloat16)
        dss = (ps * (gs - drift)).astype(jnp.bfloat16)
        dq = (contract_rows(dsd, kd) + contract_rows(dss, ks)) * score_scale
        for g in range(GROUP_HEADS):
            h = c * GROUP_HEADS + g
            dq_ref[:, h * HEAD_SIZE:(h + 1) * HEAD_SIZE] = dq[
                g * token_rows:(g + 1) * token_rows
            ].astype(dq_ref.dtype)
        doc_key = jnp.dot(dsd, q, preferred_element_type=jnp.float32) * score_scale
        doc_value = jnp.dot((pd * live).astype(jnp.bfloat16), do, preferred_element_type=jnp.float32)
        keep_ref[:, columns] = doc_key[:half]
        send_ref[:, columns] = doc_key[half:]
        keep_ref[:, value_columns] = doc_value[:half]
        send_ref[:, value_columns] = doc_value[half:]
        sk_ref[:, columns] = (
            jnp.dot(dss, q, preferred_element_type=jnp.float32) * score_scale
        ).astype(sk_ref.dtype)
        sv_ref[:, columns] = jnp.dot(
            (ps * live).astype(jnp.bfloat16), do, preferred_element_type=jnp.float32
        ).astype(sv_ref.dtype)


def per_device(
    queries,
    response_keys,
    response_values,
    document_keys,
    document_values,
    grad_out,
    lengths,
    doc_mask,
):
    token_rows = queries.shape[0]
    responses_here = lengths.shape[0]
    resp_len = token_rows // responses_here
    mask_blocks = doc_mask.shape[1]
    key_value_width = KEY_HEADS * HEAD_SIZE
    positions = jnp.arange(token_rows, dtype=jnp.int32)
    owners = positions // resp_len
    within = positions % resp_len
    live = (within < jnp.repeat(lengths, resp_len)).astype(jnp.float32)[None, :]
    spots = np.arange(token_rows)
    holders_here = spots // resp_len
    self_visible = jnp.asarray(
        (holders_here[:, None] == holders_here[None, :]) & (spots[:, None] <= spots[None, :]),
        jnp.float32,
    )
    size = lax.axis_size("resp")
    doc_mine, doc_other = gather_rows(
        jnp.concatenate([document_keys, document_values], axis=1), "resp"
    )
    slab_rows = document_keys.shape[0]
    doc_rows = size * slab_rows
    half_rows = doc_rows // 2
    block_rows = doc_rows // mask_blocks
    holders = jnp.bitwise_xor(
        lax.axis_index("resp"), jnp.asarray(np.repeat(exchange_pattern(size), slab_rows), jnp.int32)
    )
    global_rows = holders * slab_rows + jnp.asarray(np.tile(np.arange(slab_rows), size), jnp.int32)
    row_masks = jnp.repeat(doc_mask, resp_len, axis=0)
    doc_visible = (jnp.take(row_masks.T, global_rows // block_rows, axis=0) == 1).astype(
        jnp.float32
    )
    query_gradient, doc_keep, doc_send, self_key, self_value = pl.pallas_call(
        attention_kernel,
        out_shape=(
            jax.ShapeDtypeStruct(queries.shape, jnp.bfloat16),
            jax.ShapeDtypeStruct((half_rows, 2 * key_value_width), jnp.float32),
            jax.ShapeDtypeStruct((half_rows, 2 * key_value_width), jnp.float32),
            jax.ShapeDtypeStruct(response_keys.shape, jnp.bfloat16),
            jax.ShapeDtypeStruct(response_values.shape, jnp.bfloat16),
        ),
    )(
        queries,
        grad_out,
        doc_mine,
        doc_other,
        response_keys,
        response_values,
        doc_visible,
        self_visible,
        live,
    )
    summed = scatter_sum_rows(doc_keep, doc_send, "resp")
    return (
        query_gradient,
        summed[:, :key_value_width].astype(jnp.bfloat16),
        summed[:, key_value_width:].astype(jnp.bfloat16),
        self_key,
        self_value,
    )


def solution(mesh):
    return jax.shard_map(
        per_device,
        mesh=mesh,
        in_specs=(
            P(("grp", "resp"), None),
            P(("grp", "resp"), None),
            P(("grp", "resp"), None),
            P(("grp", "resp"), None),
            P(("grp", "resp"), None),
            P(("grp", "resp"), None),
            P(("grp", "resp")),
            P(("grp", "resp"), None),
        ),
        out_specs=(
            P(("grp", "resp"), None),
            P(("grp", "resp"), None),
            P(("grp", "resp"), None),
            P(("grp", "resp"), None),
            P(("grp", "resp"), None),
        ),
        check_vma=False,
    )
```

```python
import jax
import numpy as np
import jax.numpy as jnp
from jax import lax
from jax.experimental import pallas as pl
from jax.sharding import PartitionSpec as P

KEY_HEADS = 4
GROUP_HEADS = 5
HEAD_SIZE = 128


masked_score = -1e30


def exchange_bits(size):
    bits = size.bit_length() - 1
    if (1 << bits) != size:
        return None
    return bits


def swap_with(block, axis_name, size, bit):
    pairs = [(index, index ^ (1 << bit)) for index in range(size)]
    return lax.ppermute(block, axis_name, pairs)


def exchange_pattern(size):
    bits = exchange_bits(size)
    return [int(format(spot, "0%db" % bits)[::-1], 2) for spot in range(size)]


def gather_rows(blocks, axis_name):
    size = lax.axis_size(axis_name)
    bits = exchange_bits(size)
    halves = None
    for bit in reversed(range(bits)):
        if halves is not None:
            blocks = jnp.concatenate(halves)
        halves = (blocks, swap_with(blocks, axis_name, size, bit))
    return halves


def scatter_sum_rows(keep, send, axis_name):
    size = lax.axis_size(axis_name)
    bits = exchange_bits(size)
    pending = [keep]
    for bit in range(bits):
        if bit > 0:
            split = pending[0].shape[0] // 2
            send = sum(part[split:] for part in pending[1:])
            send = pending[0][split:] + send
            pending = [part[:split] for part in pending]
        pending.append(swap_with(send, axis_name, size, bit))
    return sum(pending[1:], pending[0])


def contract_rows(left, right):
    return lax.dot_general(
        left, right, (((0,), (0,)), ((), ())), preferred_element_type=jnp.float32
    )


def contract_cols(left, right):
    return lax.dot_general(
        left, right, (((1,), (1,)), ((), ())), preferred_element_type=jnp.float32
    )


def stacked_heads(ref, c):
    return jnp.concatenate(
        [
            ref[:, h * HEAD_SIZE:(h + 1) * HEAD_SIZE]
            for h in range(c * GROUP_HEADS, (c + 1) * GROUP_HEADS)
        ],
        axis=0,
    )


def attention_kernel(
    q_ref, do_ref, kva_ref, kvb_ref, ks_ref, vs_ref, vis_ref, self_ref, live_ref,
    dq_ref, keep_ref, send_ref, sk_ref, sv_ref,
):
    token_rows = q_ref.shape[0]
    width = KEY_HEADS * HEAD_SIZE
    half = kva_ref.shape[0]
    score_scale = HEAD_SIZE ** (-0.5)
    doc_seen = jnp.concatenate([vis_ref[...]] * GROUP_HEADS, axis=1) > 0.5
    self_seen = jnp.concatenate([self_ref[...]] * GROUP_HEADS, axis=1) > 0.5
    live = jnp.concatenate([live_ref[...]] * GROUP_HEADS, axis=1)
    for c in range(KEY_HEADS):
        columns = slice(c * HEAD_SIZE, (c + 1) * HEAD_SIZE)
        value_columns = slice(width + c * HEAD_SIZE, width + (c + 1) * HEAD_SIZE)
        kd = jnp.concatenate([kva_ref[:, columns], kvb_ref[:, columns]], axis=0)
        vd = jnp.concatenate([kva_ref[:, value_columns], kvb_ref[:, value_columns]], axis=0)
        ks = ks_ref[:, columns]
        vs = vs_ref[:, columns]
        q = stacked_heads(q_ref, c)
        do = stacked_heads(do_ref, c)
        sd = jnp.where(doc_seen, contract_cols(kd, q) * score_scale, masked_score)
        ss = jnp.where(self_seen, contract_cols(ks, q) * score_scale, masked_score)
        top = jnp.maximum(jnp.max(sd, axis=0, keepdims=True), jnp.max(ss, axis=0, keepdims=True))
        ed = jnp.exp(sd - top)
        es = jnp.exp(ss - top)
        total = jnp.sum(ed, axis=0, keepdims=True) + jnp.sum(es, axis=0, keepdims=True)
        weight = live / total
        pd = ed * weight
        ps = es * weight
        gd = contract_cols(vd, do)
        gs = contract_cols(vs, do)
        drift = jnp.sum(pd * gd, axis=0, keepdims=True) + jnp.sum(ps * gs, axis=0, keepdims=True)
        dsd = (pd * (gd - drift)).astype(jnp.bfloat16)
        dss = (ps * (gs - drift)).astype(jnp.bfloat16)
        dq = (contract_rows(dsd, kd) + contract_rows(dss, ks)) * score_scale
        for g in range(GROUP_HEADS):
            h = c * GROUP_HEADS + g
            dq_ref[:, h * HEAD_SIZE:(h + 1) * HEAD_SIZE] = dq[
                g * token_rows:(g + 1) * token_rows
            ].astype(dq_ref.dtype)
        doc_key = jnp.dot(dsd, q, preferred_element_type=jnp.float32) * score_scale
        doc_value = jnp.dot(pd.astype(jnp.bfloat16), do, preferred_element_type=jnp.float32)
        keep_ref[:, columns] = doc_key[:half]
        send_ref[:, columns] = doc_key[half:]
        keep_ref[:, value_columns] = doc_value[:half]
        send_ref[:, value_columns] = doc_value[half:]
        sk_ref[:, columns] = (
            jnp.dot(dss, q, preferred_element_type=jnp.float32) * score_scale
        ).astype(sk_ref.dtype)
        sv_ref[:, columns] = jnp.dot(
            ps.astype(jnp.bfloat16), do, preferred_element_type=jnp.float32
        ).astype(sv_ref.dtype)


def per_device(
    queries,
    response_keys,
    response_values,
    document_keys,
    document_values,
    grad_out,
    lengths,
    doc_mask,
):
    token_rows = queries.shape[0]
    responses_here = lengths.shape[0]
    resp_len = token_rows // responses_here
    mask_blocks = doc_mask.shape[1]
    key_value_width = KEY_HEADS * HEAD_SIZE
    positions = jnp.arange(token_rows, dtype=jnp.int32)
    owners = positions // resp_len
    within = positions % resp_len
    live = (within < jnp.repeat(lengths, resp_len)).astype(jnp.float32)[None, :]
    spots = np.arange(token_rows)
    holders_here = spots // resp_len
    self_visible = jnp.asarray(
        (holders_here[:, None] == holders_here[None, :]) & (spots[:, None] <= spots[None, :]),
        jnp.float32,
    )
    size = lax.axis_size("resp")
    doc_mine, doc_other = gather_rows(
        jnp.concatenate([document_keys, document_values], axis=1), "resp"
    )
    slab_rows = document_keys.shape[0]
    doc_rows = size * slab_rows
    half_rows = doc_rows // 2
    block_rows = doc_rows // mask_blocks
    holders = jnp.bitwise_xor(
        lax.axis_index("resp"), jnp.asarray(np.repeat(exchange_pattern(size), slab_rows), jnp.int32)
    )
    global_rows = holders * slab_rows + jnp.asarray(np.tile(np.arange(slab_rows), size), jnp.int32)
    row_masks = jnp.repeat(doc_mask, resp_len, axis=0)
    doc_visible = (jnp.take(row_masks.T, global_rows // block_rows, axis=0) == 1).astype(
        jnp.float32
    )
    query_gradient, doc_keep, doc_send, self_key, self_value = pl.pallas_call(
        attention_kernel,
        out_shape=(
            jax.ShapeDtypeStruct(queries.shape, jnp.bfloat16),
            jax.ShapeDtypeStruct((half_rows, 2 * key_value_width), jnp.float32),
            jax.ShapeDtypeStruct((half_rows, 2 * key_value_width), jnp.float32),
            jax.ShapeDtypeStruct(response_keys.shape, jnp.bfloat16),
            jax.ShapeDtypeStruct(response_values.shape, jnp.bfloat16),
        ),
    )(
        queries,
        grad_out,
        doc_mine,
        doc_other,
        response_keys,
        response_values,
        doc_visible,
        self_visible,
        live,
    )
    summed = scatter_sum_rows(doc_keep, doc_send, "resp")
    return (
        query_gradient,
        summed[:, :key_value_width].astype(jnp.bfloat16),
        summed[:, key_value_width:].astype(jnp.bfloat16),
        self_key,
        self_value,
    )


def solution(mesh):
    return jax.shard_map(
        per_device,
        mesh=mesh,
        in_specs=(
            P(("grp", "resp"), None),
            P(("grp", "resp"), None),
            P(("grp", "resp"), None),
            P(("grp", "resp"), None),
            P(("grp", "resp"), None),
            P(("grp", "resp"), None),
            P(("grp", "resp")),
            P(("grp", "resp"), None),
        ),
        out_specs=(
            P(("grp", "resp"), None),
            P(("grp", "resp"), None),
            P(("grp", "resp"), None),
            P(("grp", "resp"), None),
            P(("grp", "resp"), None),
        ),
        check_vma=False,
    )
```

```python
import jax
import numpy as np
import jax.numpy as jnp
from jax import lax
from jax.experimental import pallas as pl
from jax.sharding import PartitionSpec as P

KEY_HEADS = 4
GROUP_HEADS = 5
HEAD_SIZE = 128


masked_score = -1e30


def exchange_bits(size):
    bits = size.bit_length() - 1
    if (1 << bits) != size:
        return None
    return bits


def swap_with(block, axis_name, size, bit):
    pairs = [(index, index ^ (1 << bit)) for index in range(size)]
    return lax.ppermute(block, axis_name, pairs)


def exchange_pattern(size):
    bits = exchange_bits(size)
    return [int(format(spot, "0%db" % bits)[::-1], 2) for spot in range(size)]


def gather_rows(blocks, axis_name):
    size = lax.axis_size(axis_name)
    bits = exchange_bits(size)
    halves = None
    for bit in reversed(range(bits)):
        if halves is not None:
            blocks = jnp.concatenate(halves)
        halves = (blocks, swap_with(blocks, axis_name, size, bit))
    return halves


def scatter_sum_rows(keep, send, axis_name):
    size = lax.axis_size(axis_name)
    bits = exchange_bits(size)
    pending = [keep]
    for bit in range(bits):
        if bit > 0:
            split = pending[0].shape[0] // 2
            send = sum(part[split:] for part in pending[1:])
            send = (pending[0][split:] + send).astype(jnp.bfloat16)
            pending = [part[:split] for part in pending]
        pending.append(swap_with(send, axis_name, size, bit).astype(jnp.float32))
    return sum(pending[1:], pending[0])


def contract_rows(left, right):
    return lax.dot_general(
        left, right, (((0,), (0,)), ((), ())), preferred_element_type=jnp.float32
    )


def contract_cols(left, right):
    return lax.dot_general(
        left, right, (((1,), (1,)), ((), ())), preferred_element_type=jnp.float32
    )


def stacked_heads(ref, c):
    return jnp.concatenate(
        [
            ref[:, h * HEAD_SIZE:(h + 1) * HEAD_SIZE]
            for h in range(c * GROUP_HEADS, (c + 1) * GROUP_HEADS)
        ],
        axis=0,
    )


def attention_kernel(
    q_ref, do_ref, kva_ref, kvb_ref, ks_ref, vs_ref, vis_ref, self_ref, live_ref,
    dq_ref, keep_ref, send_ref, sk_ref, sv_ref,
):
    token_rows = q_ref.shape[0]
    width = KEY_HEADS * HEAD_SIZE
    half = kva_ref.shape[0]
    score_scale = HEAD_SIZE ** (-0.5)
    doc_seen = jnp.concatenate([vis_ref[...]] * GROUP_HEADS, axis=1) > 0.5
    self_seen = jnp.concatenate([self_ref[...]] * GROUP_HEADS, axis=1) > 0.5
    live = jnp.concatenate([live_ref[...]] * GROUP_HEADS, axis=1)
    for c in range(KEY_HEADS):
        columns = slice(c * HEAD_SIZE, (c + 1) * HEAD_SIZE)
        value_columns = slice(width + c * HEAD_SIZE, width + (c + 1) * HEAD_SIZE)
        kd = jnp.concatenate([kva_ref[:, columns], kvb_ref[:, columns]], axis=0)
        vd = jnp.concatenate([kva_ref[:, value_columns], kvb_ref[:, value_columns]], axis=0)
        ks = ks_ref[:, columns]
        vs = vs_ref[:, columns]
        q = stacked_heads(q_ref, c)
        do = stacked_heads(do_ref, c)
        sd = jnp.where(doc_seen, contract_cols(kd, q) * score_scale, masked_score)
        ss = jnp.where(self_seen, contract_cols(ks, q) * score_scale, masked_score)
        top = jnp.maximum(jnp.max(sd, axis=0, keepdims=True), jnp.max(ss, axis=0, keepdims=True))
        ed = jnp.exp(sd - top)
        es = jnp.exp(ss - top)
        total = jnp.sum(ed, axis=0, keepdims=True) + jnp.sum(es, axis=0, keepdims=True)
        weight = live / total
        pd = ed * weight
        ps = es * weight
        gd = contract_cols(vd, do)
        gs = contract_cols(vs, do)
        drift = jnp.sum(pd * gd, axis=0, keepdims=True) + jnp.sum(ps * gs, axis=0, keepdims=True)
        dsd = (pd * (gd - drift)).astype(jnp.bfloat16)
        dss = (ps * (gs - drift)).astype(jnp.bfloat16)
        dq = (contract_rows(dsd, kd) + contract_rows(dss, ks)) * score_scale
        for g in range(GROUP_HEADS):
            h = c * GROUP_HEADS + g
            dq_ref[:, h * HEAD_SIZE:(h + 1) * HEAD_SIZE] = dq[
                g * token_rows:(g + 1) * token_rows
            ].astype(dq_ref.dtype)
        doc_key = jnp.dot(dsd, q, preferred_element_type=jnp.float32) * score_scale
        doc_value = jnp.dot(pd.astype(jnp.bfloat16), do, preferred_element_type=jnp.float32)
        keep_ref[:, columns] = doc_key[:half]
        send_ref[:, columns] = doc_key[half:].astype(send_ref.dtype)
        keep_ref[:, value_columns] = doc_value[:half]
        send_ref[:, value_columns] = doc_value[half:].astype(send_ref.dtype)
        sk_ref[:, columns] = (
            jnp.dot(dss, q, preferred_element_type=jnp.float32) * score_scale
        ).astype(sk_ref.dtype)
        sv_ref[:, columns] = jnp.dot(
            ps.astype(jnp.bfloat16), do, preferred_element_type=jnp.float32
        ).astype(sv_ref.dtype)


def per_device(
    queries,
    response_keys,
    response_values,
    document_keys,
    document_values,
    grad_out,
    lengths,
    doc_mask,
):
    token_rows = queries.shape[0]
    responses_here = lengths.shape[0]
    resp_len = token_rows // responses_here
    mask_blocks = doc_mask.shape[1]
    key_value_width = KEY_HEADS * HEAD_SIZE
    positions = jnp.arange(token_rows, dtype=jnp.int32)
    owners = positions // resp_len
    within = positions % resp_len
    live = (within < jnp.repeat(lengths, resp_len)).astype(jnp.float32)[None, :]
    spots = np.arange(token_rows)
    holders_here = spots // resp_len
    self_visible = jnp.asarray(
        (holders_here[:, None] == holders_here[None, :]) & (spots[:, None] <= spots[None, :]),
        jnp.float32,
    )
    size = lax.axis_size("resp")
    doc_mine, doc_other = gather_rows(
        jnp.concatenate([document_keys, document_values], axis=1), "resp"
    )
    slab_rows = document_keys.shape[0]
    doc_rows = size * slab_rows
    half_rows = doc_rows // 2
    block_rows = doc_rows // mask_blocks
    holders = jnp.bitwise_xor(
        lax.axis_index("resp"), jnp.asarray(np.repeat(exchange_pattern(size), slab_rows), jnp.int32)
    )
    global_rows = holders * slab_rows + jnp.asarray(np.tile(np.arange(slab_rows), size), jnp.int32)
    row_masks = jnp.repeat(doc_mask, resp_len, axis=0)
    doc_visible = (jnp.take(row_masks.T, global_rows // block_rows, axis=0) == 1).astype(
        jnp.float32
    )
    query_gradient, doc_keep, doc_send, self_key, self_value = pl.pallas_call(
        attention_kernel,
        out_shape=(
            jax.ShapeDtypeStruct(queries.shape, jnp.bfloat16),
            jax.ShapeDtypeStruct((half_rows, 2 * key_value_width), jnp.float32),
            jax.ShapeDtypeStruct((half_rows, 2 * key_value_width), jnp.bfloat16),
            jax.ShapeDtypeStruct(response_keys.shape, jnp.bfloat16),
            jax.ShapeDtypeStruct(response_values.shape, jnp.bfloat16),
        ),
    )(
        queries,
        grad_out,
        doc_mine,
        doc_other,
        response_keys,
        response_values,
        doc_visible,
        self_visible,
        live,
    )
    summed = scatter_sum_rows(doc_keep, doc_send, "resp")
    return (
        query_gradient,
        summed[:, :key_value_width].astype(jnp.bfloat16),
        summed[:, key_value_width:].astype(jnp.bfloat16),
        self_key,
        self_value,
    )


def solution(mesh):
    return jax.shard_map(
        per_device,
        mesh=mesh,
        in_specs=(
            P(("grp", "resp"), None),
            P(("grp", "resp"), None),
            P(("grp", "resp"), None),
            P(("grp", "resp"), None),
            P(("grp", "resp"), None),
            P(("grp", "resp"), None),
            P(("grp", "resp")),
            P(("grp", "resp"), None),
        ),
        out_specs=(
            P(("grp", "resp"), None),
            P(("grp", "resp"), None),
            P(("grp", "resp"), None),
            P(("grp", "resp"), None),
            P(("grp", "resp"), None),
        ),
        check_vma=False,
    )
```

```python
import jax
import numpy as np
import jax.numpy as jnp
from jax import lax
from jax.experimental import pallas as pl
from jax.sharding import PartitionSpec as P

KEY_HEADS = 4
GROUP_HEADS = 5
HEAD_SIZE = 128


masked_score = -1e30


def exchange_bits(size):
    bits = size.bit_length() - 1
    if (1 << bits) != size:
        return None
    return bits


def swap_with(block, axis_name, size, bit):
    pairs = [(index, index ^ (1 << bit)) for index in range(size)]
    return lax.ppermute(block, axis_name, pairs)


def exchange_pattern(size):
    bits = exchange_bits(size)
    return [int(format(spot, "0%db" % bits)[::-1], 2) for spot in range(size)]


def gather_rows(blocks, axis_name):
    size = lax.axis_size(axis_name)
    bits = exchange_bits(size)
    halves = None
    for bit in reversed(range(bits)):
        if halves is not None:
            blocks = jnp.concatenate(halves)
        halves = (blocks, swap_with(blocks, axis_name, size, bit))
    return halves


def scatter_sum_rows(keep, send, axis_name):
    size = lax.axis_size(axis_name)
    bits = exchange_bits(size)
    pending = [keep]
    for bit in range(bits):
        if bit > 0:
            split = pending[0].shape[2] // 2
            send = sum(part[:, :, split:] for part in pending[1:])
            send = pending[0][:, :, split:] + send
            pending = [part[:, :, :split] for part in pending]
        pending.append(swap_with(send, axis_name, size, bit))
    return sum(pending[1:], pending[0])


def contract_rows(left, right):
    return lax.dot_general(
        left, right, (((0,), (0,)), ((), ())), preferred_element_type=jnp.float32
    )


def contract_cols(left, right):
    return lax.dot_general(
        left, right, (((1,), (1,)), ((), ())), preferred_element_type=jnp.float32
    )


def stacked_heads(ref, c):
    return jnp.concatenate(
        [
            ref[:, h * HEAD_SIZE:(h + 1) * HEAD_SIZE]
            for h in range(c * GROUP_HEADS, (c + 1) * GROUP_HEADS)
        ],
        axis=0,
    )


def attention_kernel(
    q_ref, do_ref, ka_ref, va_ref, kb_ref, vb_ref, ks_ref, vs_ref, vis_ref, self_ref, live_ref,
    dq_ref, keep_ref, send_ref, sk_ref, sv_ref,
):
    token_rows = q_ref.shape[0]
    half = ka_ref.shape[0]
    score_scale = HEAD_SIZE ** (-0.5)
    doc_seen = jnp.concatenate([vis_ref[...]] * GROUP_HEADS, axis=1) > 0.5
    self_seen = jnp.concatenate([self_ref[...]] * GROUP_HEADS, axis=1) > 0.5
    live = jnp.concatenate([live_ref[...]] * GROUP_HEADS, axis=1)
    kd = jnp.concatenate([ka_ref[...], kb_ref[...]], axis=0)
    vd = jnp.concatenate([va_ref[...], vb_ref[...]], axis=0)
    ks = ks_ref[...]
    vs = vs_ref[...]
    q = jnp.concatenate(
        [q_ref[:, g * HEAD_SIZE:(g + 1) * HEAD_SIZE] for g in range(GROUP_HEADS)], axis=0
    )
    do = jnp.concatenate(
        [do_ref[:, g * HEAD_SIZE:(g + 1) * HEAD_SIZE] for g in range(GROUP_HEADS)], axis=0
    )
    sd = jnp.where(doc_seen, contract_cols(kd, q) * score_scale, masked_score)
    ss = jnp.where(self_seen, contract_cols(ks, q) * score_scale, masked_score)
    top = jnp.maximum(jnp.max(sd, axis=0, keepdims=True), jnp.max(ss, axis=0, keepdims=True))
    ed = jnp.exp(sd - top)
    es = jnp.exp(ss - top)
    total = jnp.sum(ed, axis=0, keepdims=True) + jnp.sum(es, axis=0, keepdims=True)
    weight = live / total
    pd = ed * weight
    ps = es * weight
    gd = contract_cols(vd, do)
    gs = contract_cols(vs, do)
    drift = jnp.sum(pd * gd, axis=0, keepdims=True) + jnp.sum(ps * gs, axis=0, keepdims=True)
    dsd = (pd * (gd - drift)).astype(jnp.bfloat16)
    dss = (ps * (gs - drift)).astype(jnp.bfloat16)
    dq = (contract_rows(dsd, kd) + contract_rows(dss, ks)) * score_scale
    for g in range(GROUP_HEADS):
        dq_ref[:, g * HEAD_SIZE:(g + 1) * HEAD_SIZE] = dq[
            g * token_rows:(g + 1) * token_rows
        ].astype(dq_ref.dtype)
    doc_key = jnp.dot(dsd, q, preferred_element_type=jnp.float32) * score_scale
    doc_value = jnp.dot(pd.astype(jnp.bfloat16), do, preferred_element_type=jnp.float32)
    keep_ref[0, 0] = doc_key[:half]
    send_ref[0, 0] = doc_key[half:]
    keep_ref[0, 1] = doc_value[:half]
    send_ref[0, 1] = doc_value[half:]
    sk_ref[...] = (jnp.dot(dss, q, preferred_element_type=jnp.float32) * score_scale).astype(
        sk_ref.dtype
    )
    sv_ref[...] = jnp.dot(
        ps.astype(jnp.bfloat16), do, preferred_element_type=jnp.float32
    ).astype(sv_ref.dtype)


def per_device(
    queries,
    response_keys,
    response_values,
    document_keys,
    document_values,
    grad_out,
    lengths,
    doc_mask,
):
    token_rows = queries.shape[0]
    responses_here = lengths.shape[0]
    resp_len = token_rows // responses_here
    mask_blocks = doc_mask.shape[1]
    key_value_width = KEY_HEADS * HEAD_SIZE
    positions = jnp.arange(token_rows, dtype=jnp.int32)
    owners = positions // resp_len
    within = positions % resp_len
    live = (within < jnp.repeat(lengths, resp_len)).astype(jnp.float32)[None, :]
    spots = np.arange(token_rows)
    holders_here = spots // resp_len
    self_visible = jnp.asarray(
        (holders_here[:, None] == holders_here[None, :]) & (spots[:, None] <= spots[None, :]),
        jnp.float32,
    )
    size = lax.axis_size("resp")
    doc_mine, doc_other = gather_rows(
        jnp.concatenate([document_keys, document_values], axis=1), "resp"
    )
    slab_rows = document_keys.shape[0]
    doc_rows = size * slab_rows
    half_rows = doc_rows // 2
    block_rows = doc_rows // mask_blocks
    holders = jnp.bitwise_xor(
        lax.axis_index("resp"), jnp.asarray(np.repeat(exchange_pattern(size), slab_rows), jnp.int32)
    )
    global_rows = holders * slab_rows + jnp.asarray(np.tile(np.arange(slab_rows), size), jnp.int32)
    row_masks = jnp.repeat(doc_mask, resp_len, axis=0)
    doc_visible = (jnp.take(row_masks.T, global_rows // block_rows, axis=0) == 1).astype(
        jnp.float32
    )
    head_block = GROUP_HEADS * HEAD_SIZE
    part_shape = (KEY_HEADS, 2, half_rows, HEAD_SIZE)
    part_spec = pl.BlockSpec((1, 2, half_rows, HEAD_SIZE), lambda c: (c, 0, 0, 0))
    query_gradient, doc_keep, doc_send, self_key, self_value = pl.pallas_call(
        attention_kernel,
        grid=(KEY_HEADS,),
        in_specs=[
            pl.BlockSpec((token_rows, head_block), lambda c: (0, c)),
            pl.BlockSpec((token_rows, head_block), lambda c: (0, c)),
            pl.BlockSpec((half_rows, HEAD_SIZE), lambda c: (0, c)),
            pl.BlockSpec((half_rows, HEAD_SIZE), lambda c: (0, c + KEY_HEADS)),
            pl.BlockSpec((half_rows, HEAD_SIZE), lambda c: (0, c)),
            pl.BlockSpec((half_rows, HEAD_SIZE), lambda c: (0, c + KEY_HEADS)),
            pl.BlockSpec((token_rows, HEAD_SIZE), lambda c: (0, c)),
            pl.BlockSpec((token_rows, HEAD_SIZE), lambda c: (0, c)),
            pl.BlockSpec((doc_rows, token_rows), lambda c: (0, 0)),
            pl.BlockSpec((token_rows, token_rows), lambda c: (0, 0)),
            pl.BlockSpec((1, token_rows), lambda c: (0, 0)),
        ],
        out_specs=[
            pl.BlockSpec((token_rows, head_block), lambda c: (0, c)),
            part_spec,
            part_spec,
            pl.BlockSpec((token_rows, HEAD_SIZE), lambda c: (0, c)),
            pl.BlockSpec((token_rows, HEAD_SIZE), lambda c: (0, c)),
        ],
        out_shape=(
            jax.ShapeDtypeStruct(queries.shape, jnp.bfloat16),
            jax.ShapeDtypeStruct(part_shape, jnp.float32),
            jax.ShapeDtypeStruct(part_shape, jnp.float32),
            jax.ShapeDtypeStruct(response_keys.shape, jnp.bfloat16),
            jax.ShapeDtypeStruct(response_values.shape, jnp.bfloat16),
        ),
    )(
        queries,
        grad_out,
        doc_mine,
        doc_mine,
        doc_other,
        doc_other,
        response_keys,
        response_values,
        doc_visible,
        self_visible,
        live,
    )
    summed = scatter_sum_rows(doc_keep, doc_send, "resp")
    doc_grads = jnp.transpose(summed, (1, 2, 0, 3)).reshape(2, slab_rows, key_value_width)
    return (
        query_gradient,
        doc_grads[0].astype(jnp.bfloat16),
        doc_grads[1].astype(jnp.bfloat16),
        self_key,
        self_value,
    )


def solution(mesh):
    return jax.shard_map(
        per_device,
        mesh=mesh,
        in_specs=(
            P(("grp", "resp"), None),
            P(("grp", "resp"), None),
            P(("grp", "resp"), None),
            P(("grp", "resp"), None),
            P(("grp", "resp"), None),
            P(("grp", "resp"), None),
            P(("grp", "resp")),
            P(("grp", "resp"), None),
        ),
        out_specs=(
            P(("grp", "resp"), None),
            P(("grp", "resp"), None),
            P(("grp", "resp"), None),
            P(("grp", "resp"), None),
            P(("grp", "resp"), None),
        ),
        check_vma=False,
    )
```

```python
import jax
import numpy as np
import jax.numpy as jnp
from jax import lax
from jax.experimental import pallas as pl
from jax.sharding import PartitionSpec as P

KEY_HEADS = 4
GROUP_HEADS = 5
HEAD_SIZE = 128


masked_score = -1e30


def exchange_bits(size):
    bits = size.bit_length() - 1
    if (1 << bits) != size:
        return None
    return bits


def swap_with(block, axis_name, size, bit):
    pairs = [(index, index ^ (1 << bit)) for index in range(size)]
    return lax.ppermute(block, axis_name, pairs)


def exchange_pattern(size):
    bits = exchange_bits(size)
    return [int(format(spot, "0%db" % bits)[::-1], 2) for spot in range(size)]


def gather_rows(blocks, axis_name):
    size = lax.axis_size(axis_name)
    bits = exchange_bits(size)
    halves = None
    for bit in reversed(range(bits)):
        if halves is not None:
            blocks = jnp.concatenate(halves)
        halves = (blocks, swap_with(blocks, axis_name, size, bit))
    return halves


def scatter_sum_rows(keep, send, axis_name):
    size = lax.axis_size(axis_name)
    bits = exchange_bits(size)
    pending = [keep]
    for bit in range(bits):
        if bit > 0:
            split = pending[0].shape[0] // 2
            send = sum(part[split:] for part in pending[1:])
            send = pending[0][split:] + send
            pending = [part[:split] for part in pending]
        pending.append(swap_with(send, axis_name, size, bit))
    return sum(pending[1:], pending[0])


def contract_rows(left, right):
    return lax.dot_general(
        left, right, (((0,), (0,)), ((), ())), preferred_element_type=jnp.float32
    )


def contract_cols(left, right):
    return lax.dot_general(
        left, right, (((1,), (1,)), ((), ())), preferred_element_type=jnp.float32
    )


def stacked_heads(ref, c):
    return jnp.concatenate(
        [
            ref[:, h * HEAD_SIZE:(h + 1) * HEAD_SIZE]
            for h in range(c * GROUP_HEADS, (c + 1) * GROUP_HEADS)
        ],
        axis=0,
    )


def attention_kernel(
    q_ref, do_ref, kva_ref, kvb_ref, ks_ref, vs_ref, vis_ref, self_ref, live_ref,
    dq_ref, keep_ref, send_ref, sk_ref, sv_ref,
):
    width = KEY_HEADS * HEAD_SIZE
    half = kva_ref.shape[0]
    doc_rows = 2 * half
    score_scale = HEAD_SIZE ** (-0.5)
    seen = jnp.concatenate([vis_ref[...], self_ref[...]], axis=0) > 0.5
    live = live_ref[...]
    for c in range(KEY_HEADS):
        columns = slice(c * HEAD_SIZE, (c + 1) * HEAD_SIZE)
        value_columns = slice(width + c * HEAD_SIZE, width + (c + 1) * HEAD_SIZE)
        keys = jnp.concatenate(
            [kva_ref[:, columns], kvb_ref[:, columns], ks_ref[:, columns]], axis=0
        )
        values = jnp.concatenate(
            [kva_ref[:, value_columns], kvb_ref[:, value_columns], vs_ref[:, columns]], axis=0
        )
        key_total = jnp.zeros(keys.shape, jnp.float32)
        value_total = jnp.zeros(keys.shape, jnp.float32)
        for g in range(GROUP_HEADS):
            h = c * GROUP_HEADS + g
            head = slice(h * HEAD_SIZE, (h + 1) * HEAD_SIZE)
            q = q_ref[:, head]
            do = do_ref[:, head]
            score = jnp.where(seen, contract_cols(keys, q) * score_scale, masked_score)
            top = jnp.max(score, axis=0, keepdims=True)
            grown = jnp.exp(score - top)
            prob = grown * (live / jnp.sum(grown, axis=0, keepdims=True))
            slope = contract_cols(values, do)
            drift = jnp.sum(prob * slope, axis=0, keepdims=True)
            dscore = (prob * (slope - drift)).astype(jnp.bfloat16)
            dq_ref[:, head] = (contract_rows(dscore, keys) * score_scale).astype(dq_ref.dtype)
            key_total = key_total + jnp.dot(dscore, q, preferred_element_type=jnp.float32)
            value_total = value_total + jnp.dot(
                prob.astype(jnp.bfloat16), do, preferred_element_type=jnp.float32
            )
        key_total = key_total * score_scale
        keep_ref[:, columns] = key_total[:half]
        send_ref[:, columns] = key_total[half:doc_rows]
        keep_ref[:, value_columns] = value_total[:half]
        send_ref[:, value_columns] = value_total[half:doc_rows]
        sk_ref[:, columns] = key_total[doc_rows:].astype(sk_ref.dtype)
        sv_ref[:, columns] = value_total[doc_rows:].astype(sv_ref.dtype)


def per_device(
    queries,
    response_keys,
    response_values,
    document_keys,
    document_values,
    grad_out,
    lengths,
    doc_mask,
):
    token_rows = queries.shape[0]
    responses_here = lengths.shape[0]
    resp_len = token_rows // responses_here
    mask_blocks = doc_mask.shape[1]
    key_value_width = KEY_HEADS * HEAD_SIZE
    positions = jnp.arange(token_rows, dtype=jnp.int32)
    owners = positions // resp_len
    within = positions % resp_len
    live = (within < jnp.repeat(lengths, resp_len)).astype(jnp.float32)[None, :]
    spots = np.arange(token_rows)
    holders_here = spots // resp_len
    self_visible = jnp.asarray(
        (holders_here[:, None] == holders_here[None, :]) & (spots[:, None] <= spots[None, :]),
        jnp.float32,
    )
    size = lax.axis_size("resp")
    doc_mine, doc_other = gather_rows(
        jnp.concatenate([document_keys, document_values], axis=1), "resp"
    )
    slab_rows = document_keys.shape[0]
    doc_rows = size * slab_rows
    half_rows = doc_rows // 2
    block_rows = doc_rows // mask_blocks
    holders = jnp.bitwise_xor(
        lax.axis_index("resp"), jnp.asarray(np.repeat(exchange_pattern(size), slab_rows), jnp.int32)
    )
    global_rows = holders * slab_rows + jnp.asarray(np.tile(np.arange(slab_rows), size), jnp.int32)
    row_masks = jnp.repeat(doc_mask, resp_len, axis=0)
    doc_visible = (jnp.take(row_masks.T, global_rows // block_rows, axis=0) == 1).astype(
        jnp.float32
    )
    query_gradient, doc_keep, doc_send, self_key, self_value = pl.pallas_call(
        attention_kernel,
        out_shape=(
            jax.ShapeDtypeStruct(queries.shape, jnp.bfloat16),
            jax.ShapeDtypeStruct((half_rows, 2 * key_value_width), jnp.float32),
            jax.ShapeDtypeStruct((half_rows, 2 * key_value_width), jnp.float32),
            jax.ShapeDtypeStruct(response_keys.shape, jnp.bfloat16),
            jax.ShapeDtypeStruct(response_values.shape, jnp.bfloat16),
        ),
    )(
        queries,
        grad_out,
        doc_mine,
        doc_other,
        response_keys,
        response_values,
        doc_visible,
        self_visible,
        live,
    )
    summed = scatter_sum_rows(doc_keep, doc_send, "resp")
    return (
        query_gradient,
        summed[:, :key_value_width].astype(jnp.bfloat16),
        summed[:, key_value_width:].astype(jnp.bfloat16),
        self_key,
        self_value,
    )


def solution(mesh):
    return jax.shard_map(
        per_device,
        mesh=mesh,
        in_specs=(
            P(("grp", "resp"), None),
            P(("grp", "resp"), None),
            P(("grp", "resp"), None),
            P(("grp", "resp"), None),
            P(("grp", "resp"), None),
            P(("grp", "resp"), None),
            P(("grp", "resp")),
            P(("grp", "resp"), None),
        ),
        out_specs=(
            P(("grp", "resp"), None),
            P(("grp", "resp"), None),
            P(("grp", "resp"), None),
            P(("grp", "resp"), None),
            P(("grp", "resp"), None),
        ),
        check_vma=False,
    )
```

```python
import jax
import numpy as np
import jax.numpy as jnp
from jax import lax
from jax.experimental import pallas as pl
from jax.sharding import PartitionSpec as P

KEY_HEADS = 4
GROUP_HEADS = 5
HEAD_SIZE = 128


masked_score = -1e30


def exchange_bits(size):
    bits = size.bit_length() - 1
    if (1 << bits) != size:
        return None
    return bits


def swap_with(block, axis_name, size, bit):
    pairs = [(index, index ^ (1 << bit)) for index in range(size)]
    return lax.ppermute(block, axis_name, pairs)


def exchange_pattern(size):
    bits = exchange_bits(size)
    return [int(format(spot, "0%db" % bits)[::-1], 2) for spot in range(size)]


def gather_rows(blocks, axis_name):
    size = lax.axis_size(axis_name)
    bits = exchange_bits(size)
    halves = None
    for bit in reversed(range(bits)):
        if halves is not None:
            blocks = jnp.concatenate(halves)
        halves = (blocks, swap_with(blocks, axis_name, size, bit))
    return halves


def scatter_sum_rows(keep, send, axis_name):
    size = lax.axis_size(axis_name)
    bits = exchange_bits(size)
    pending = [keep]
    for bit in range(bits):
        if bit > 0:
            split = pending[0].shape[0] // 2
            send = sum(part[split:] for part in pending[1:])
            send = pending[0][split:] + send
            pending = [part[:split] for part in pending]
        pending.append(swap_with(send, axis_name, size, bit))
    return sum(pending[1:], pending[0])


def contract_rows(left, right):
    return lax.dot_general(
        left, right, (((0,), (0,)), ((), ())), preferred_element_type=jnp.float32
    )


def contract_cols(left, right):
    return lax.dot_general(
        left, right, (((1,), (1,)), ((), ())), preferred_element_type=jnp.float32
    )


def stacked_heads(ref, c):
    return jnp.concatenate(
        [
            ref[:, h * HEAD_SIZE:(h + 1) * HEAD_SIZE]
            for h in range(c * GROUP_HEADS, (c + 1) * GROUP_HEADS)
        ],
        axis=0,
    )


def attention_kernel(
    q_ref, do_ref, kva_ref, kvb_ref, ks_ref, vs_ref, vis_ref, self_ref, live_ref,
    dq_ref, keep_ref, send_ref, sk_ref, sv_ref,
):
    token_rows = q_ref.shape[0]
    width = KEY_HEADS * HEAD_SIZE
    half = kva_ref.shape[0]
    doc_rows = 2 * half
    score_scale = HEAD_SIZE ** (-0.5)
    seen = jnp.concatenate(
        [jnp.concatenate([vis_ref[...], self_ref[...]], axis=0)] * GROUP_HEADS, axis=1
    ) > 0.5
    live = jnp.concatenate([live_ref[...]] * GROUP_HEADS, axis=1)
    for c in range(KEY_HEADS):
        columns = slice(c * HEAD_SIZE, (c + 1) * HEAD_SIZE)
        value_columns = slice(width + c * HEAD_SIZE, width + (c + 1) * HEAD_SIZE)
        keys = jnp.concatenate(
            [kva_ref[:, columns], kvb_ref[:, columns], ks_ref[:, columns]], axis=0
        )
        values = jnp.concatenate(
            [kva_ref[:, value_columns], kvb_ref[:, value_columns], vs_ref[:, columns]], axis=0
        )
        q = stacked_heads(q_ref, c)
        do = stacked_heads(do_ref, c)
        score = jnp.where(seen, contract_cols(keys, q) * score_scale, masked_score)
        top = jnp.max(score, axis=0, keepdims=True)
        grown = jnp.exp(score - top)
        prob = grown * (live / jnp.sum(grown, axis=0, keepdims=True))
        slope = contract_cols(values, do)
        drift = jnp.sum(prob * slope, axis=0, keepdims=True)
        dscore = (prob * (slope - drift)).astype(jnp.bfloat16)
        dq = contract_rows(dscore, keys) * score_scale
        for g in range(GROUP_HEADS):
            h = c * GROUP_HEADS + g
            dq_ref[:, h * HEAD_SIZE:(h + 1) * HEAD_SIZE] = dq[
                g * token_rows:(g + 1) * token_rows
            ].astype(dq_ref.dtype)
        key_total = jnp.dot(dscore, q, preferred_element_type=jnp.float32) * score_scale
        value_total = jnp.dot(prob.astype(jnp.bfloat16), do, preferred_element_type=jnp.float32)
        keep_ref[:, columns] = key_total[:half]
        send_ref[:, columns] = key_total[half:doc_rows]
        keep_ref[:, value_columns] = value_total[:half]
        send_ref[:, value_columns] = value_total[half:doc_rows]
        sk_ref[:, columns] = key_total[doc_rows:].astype(sk_ref.dtype)
        sv_ref[:, columns] = value_total[doc_rows:].astype(sv_ref.dtype)


def per_device(
    queries,
    response_keys,
    response_values,
    document_keys,
    document_values,
    grad_out,
    lengths,
    doc_mask,
):
    token_rows = queries.shape[0]
    responses_here = lengths.shape[0]
    resp_len = token_rows // responses_here
    mask_blocks = doc_mask.shape[1]
    key_value_width = KEY_HEADS * HEAD_SIZE
    positions = jnp.arange(token_rows, dtype=jnp.int32)
    owners = positions // resp_len
    within = positions % resp_len
    live = (within < jnp.repeat(lengths, resp_len)).astype(jnp.float32)[None, :]
    spots = np.arange(token_rows)
    holders_here = spots // resp_len
    self_visible = jnp.asarray(
        (holders_here[:, None] == holders_here[None, :]) & (spots[:, None] <= spots[None, :]),
        jnp.float32,
    )
    size = lax.axis_size("resp")
    doc_mine, doc_other = gather_rows(
        jnp.concatenate([document_keys, document_values], axis=1), "resp"
    )
    slab_rows = document_keys.shape[0]
    doc_rows = size * slab_rows
    half_rows = doc_rows // 2
    block_rows = doc_rows // mask_blocks
    holders = jnp.bitwise_xor(
        lax.axis_index("resp"), jnp.asarray(np.repeat(exchange_pattern(size), slab_rows), jnp.int32)
    )
    global_rows = holders * slab_rows + jnp.asarray(np.tile(np.arange(slab_rows), size), jnp.int32)
    row_masks = jnp.repeat(doc_mask, resp_len, axis=0)
    doc_visible = (jnp.take(row_masks.T, global_rows // block_rows, axis=0) == 1).astype(
        jnp.float32
    )
    query_gradient, doc_keep, doc_send, self_key, self_value = pl.pallas_call(
        attention_kernel,
        out_shape=(
            jax.ShapeDtypeStruct(queries.shape, jnp.bfloat16),
            jax.ShapeDtypeStruct((half_rows, 2 * key_value_width), jnp.float32),
            jax.ShapeDtypeStruct((half_rows, 2 * key_value_width), jnp.float32),
            jax.ShapeDtypeStruct(response_keys.shape, jnp.bfloat16),
            jax.ShapeDtypeStruct(response_values.shape, jnp.bfloat16),
        ),
    )(
        queries,
        grad_out,
        doc_mine,
        doc_other,
        response_keys,
        response_values,
        doc_visible,
        self_visible,
        live,
    )
    summed = scatter_sum_rows(doc_keep, doc_send, "resp")
    return (
        query_gradient,
        summed[:, :key_value_width].astype(jnp.bfloat16),
        summed[:, key_value_width:].astype(jnp.bfloat16),
        self_key,
        self_value,
    )


def solution(mesh):
    return jax.shard_map(
        per_device,
        mesh=mesh,
        in_specs=(
            P(("grp", "resp"), None),
            P(("grp", "resp"), None),
            P(("grp", "resp"), None),
            P(("grp", "resp"), None),
            P(("grp", "resp"), None),
            P(("grp", "resp"), None),
            P(("grp", "resp")),
            P(("grp", "resp"), None),
        ),
        out_specs=(
            P(("grp", "resp"), None),
            P(("grp", "resp"), None),
            P(("grp", "resp"), None),
            P(("grp", "resp"), None),
            P(("grp", "resp"), None),
        ),
        check_vma=False,
    )
```

```python
import jax
import numpy as np
import jax.numpy as jnp
from jax import lax
from jax.experimental import pallas as pl
from jax.sharding import PartitionSpec as P

KEY_HEADS = 4
GROUP_HEADS = 5
HEAD_SIZE = 128


masked_score = -1e30


def exchange_bits(size):
    bits = size.bit_length() - 1
    if (1 << bits) != size:
        return None
    return bits


def swap_with(block, axis_name, size, bit):
    pairs = [(index, index ^ (1 << bit)) for index in range(size)]
    return lax.ppermute(block, axis_name, pairs)


def exchange_pattern(size):
    bits = exchange_bits(size)
    return [int(format(spot, "0%db" % bits)[::-1], 2) for spot in range(size)]


def gather_rows(blocks, axis_name):
    size = lax.axis_size(axis_name)
    bits = exchange_bits(size)
    halves = None
    for bit in reversed(range(bits)):
        if halves is not None:
            blocks = jnp.concatenate(halves)
        halves = (blocks, swap_with(blocks, axis_name, size, bit))
    return halves


def scatter_sum_rows(keep, send, axis_name):
    size = lax.axis_size(axis_name)
    bits = exchange_bits(size)
    pending = [keep]
    for bit in range(bits):
        if bit > 0:
            split = pending[0].shape[0] // 2
            send = sum(part[split:] for part in pending[1:])
            send = pending[0][split:] + send
            pending = [part[:split] for part in pending]
        if bit in (1, 2):
            send = swap_with(send.astype(jnp.bfloat16), axis_name, size, bit).astype(jnp.float32)
        else:
            send = swap_with(send, axis_name, size, bit)
        pending.append(send)
    return sum(pending[1:], pending[0])


def contract_rows(left, right):
    return lax.dot_general(
        left, right, (((0,), (0,)), ((), ())), preferred_element_type=jnp.float32
    )


def contract_cols(left, right):
    return lax.dot_general(
        left, right, (((1,), (1,)), ((), ())), preferred_element_type=jnp.float32
    )


def stacked_heads(ref, c):
    return jnp.concatenate(
        [
            ref[:, h * HEAD_SIZE:(h + 1) * HEAD_SIZE]
            for h in range(c * GROUP_HEADS, (c + 1) * GROUP_HEADS)
        ],
        axis=0,
    )


def attention_kernel(
    q_ref, do_ref, kva_ref, kvb_ref, ks_ref, vs_ref, vis_ref, self_ref, live_ref,
    dq_ref, keep_ref, send_ref, sk_ref, sv_ref,
):
    token_rows = q_ref.shape[0]
    width = KEY_HEADS * HEAD_SIZE
    half = kva_ref.shape[0]
    doc_rows = 2 * half
    score_scale = HEAD_SIZE ** (-0.5)
    seen = jnp.concatenate(
        [jnp.concatenate([vis_ref[...], self_ref[...]], axis=0)] * GROUP_HEADS, axis=1
    ) > 0.5
    live = jnp.concatenate([live_ref[...]] * GROUP_HEADS, axis=1)
    for c in range(KEY_HEADS):
        columns = slice(c * HEAD_SIZE, (c + 1) * HEAD_SIZE)
        value_columns = slice(width + c * HEAD_SIZE, width + (c + 1) * HEAD_SIZE)
        keys = jnp.concatenate(
            [kva_ref[:, columns], kvb_ref[:, columns], ks_ref[:, columns]], axis=0
        )
        values = jnp.concatenate(
            [kva_ref[:, value_columns], kvb_ref[:, value_columns], vs_ref[:, columns]], axis=0
        )
        q = stacked_heads(q_ref, c)
        do = stacked_heads(do_ref, c)
        score = jnp.where(seen, contract_cols(keys, q) * score_scale, masked_score)
        top = jnp.max(score, axis=0, keepdims=True)
        grown = jnp.exp(score - top)
        prob = grown * (live / jnp.sum(grown, axis=0, keepdims=True))
        slope = contract_cols(values, do)
        drift = jnp.sum(prob * slope, axis=0, keepdims=True)
        dscore = (prob * (slope - drift)).astype(jnp.bfloat16)
        dq = contract_rows(dscore, keys) * score_scale
        for g in range(GROUP_HEADS):
            h = c * GROUP_HEADS + g
            dq_ref[:, h * HEAD_SIZE:(h + 1) * HEAD_SIZE] = dq[
                g * token_rows:(g + 1) * token_rows
            ].astype(dq_ref.dtype)
        key_total = jnp.dot(dscore, q, preferred_element_type=jnp.float32) * score_scale
        value_total = jnp.dot(prob.astype(jnp.bfloat16), do, preferred_element_type=jnp.float32)
        keep_ref[:, columns] = key_total[:half]
        send_ref[:, columns] = key_total[half:doc_rows]
        keep_ref[:, value_columns] = value_total[:half]
        send_ref[:, value_columns] = value_total[half:doc_rows]
        sk_ref[:, columns] = key_total[doc_rows:].astype(sk_ref.dtype)
        sv_ref[:, columns] = value_total[doc_rows:].astype(sv_ref.dtype)


def per_device(
    queries,
    response_keys,
    response_values,
    document_keys,
    document_values,
    grad_out,
    lengths,
    doc_mask,
):
    token_rows = queries.shape[0]
    responses_here = lengths.shape[0]
    resp_len = token_rows // responses_here
    mask_blocks = doc_mask.shape[1]
    key_value_width = KEY_HEADS * HEAD_SIZE
    positions = jnp.arange(token_rows, dtype=jnp.int32)
    owners = positions // resp_len
    within = positions % resp_len
    live = (within < jnp.repeat(lengths, resp_len)).astype(jnp.float32)[None, :]
    spots = np.arange(token_rows)
    holders_here = spots // resp_len
    self_visible = jnp.asarray(
        (holders_here[:, None] == holders_here[None, :]) & (spots[:, None] <= spots[None, :]),
        jnp.float32,
    )
    size = lax.axis_size("resp")
    doc_mine, doc_other = gather_rows(
        jnp.concatenate([document_keys, document_values], axis=1), "resp"
    )
    slab_rows = document_keys.shape[0]
    doc_rows = size * slab_rows
    half_rows = doc_rows // 2
    block_rows = doc_rows // mask_blocks
    holders = jnp.bitwise_xor(
        lax.axis_index("resp"), jnp.asarray(np.repeat(exchange_pattern(size), slab_rows), jnp.int32)
    )
    global_rows = holders * slab_rows + jnp.asarray(np.tile(np.arange(slab_rows), size), jnp.int32)
    row_masks = jnp.repeat(doc_mask, resp_len, axis=0)
    doc_visible = (jnp.take(row_masks.T, global_rows // block_rows, axis=0) == 1).astype(
        jnp.float32
    )
    query_gradient, doc_keep, doc_send, self_key, self_value = pl.pallas_call(
        attention_kernel,
        out_shape=(
            jax.ShapeDtypeStruct(queries.shape, jnp.bfloat16),
            jax.ShapeDtypeStruct((half_rows, 2 * key_value_width), jnp.float32),
            jax.ShapeDtypeStruct((half_rows, 2 * key_value_width), jnp.float32),
            jax.ShapeDtypeStruct(response_keys.shape, jnp.bfloat16),
            jax.ShapeDtypeStruct(response_values.shape, jnp.bfloat16),
        ),
    )(
        queries,
        grad_out,
        doc_mine,
        doc_other,
        response_keys,
        response_values,
        doc_visible,
        self_visible,
        live,
    )
    summed = scatter_sum_rows(doc_keep, doc_send, "resp")
    return (
        query_gradient,
        summed[:, :key_value_width].astype(jnp.bfloat16),
        summed[:, key_value_width:].astype(jnp.bfloat16),
        self_key,
        self_value,
    )


def solution(mesh):
    return jax.shard_map(
        per_device,
        mesh=mesh,
        in_specs=(
            P(("grp", "resp"), None),
            P(("grp", "resp"), None),
            P(("grp", "resp"), None),
            P(("grp", "resp"), None),
            P(("grp", "resp"), None),
            P(("grp", "resp"), None),
            P(("grp", "resp")),
            P(("grp", "resp"), None),
        ),
        out_specs=(
            P(("grp", "resp"), None),
            P(("grp", "resp"), None),
            P(("grp", "resp"), None),
            P(("grp", "resp"), None),
            P(("grp", "resp"), None),
        ),
        check_vma=False,
    )
```

```python
import jax
import numpy as np
import jax.numpy as jnp
from jax import lax
from jax.experimental import pallas as pl
from jax.sharding import PartitionSpec as P

KEY_HEADS = 4
GROUP_HEADS = 5
HEAD_SIZE = 128


masked_score = -1e30


def exchange_bits(size):
    bits = size.bit_length() - 1
    if (1 << bits) != size:
        return None
    return bits


def swap_with(block, axis_name, size, bit):
    pairs = [(index, index ^ (1 << bit)) for index in range(size)]
    return lax.ppermute(block, axis_name, pairs)


def exchange_pattern(size):
    bits = exchange_bits(size)
    return [int(format(spot, "0%db" % bits)[::-1], 2) for spot in range(size)]


def gather_rows(blocks, axis_name):
    size = lax.axis_size(axis_name)
    bits = exchange_bits(size)
    halves = None
    for bit in reversed(range(bits)):
        if halves is not None:
            blocks = jnp.concatenate(halves)
        halves = (blocks, swap_with(blocks, axis_name, size, bit))
    return halves


def scatter_sum_rows(keep, send, axis_name):
    size = lax.axis_size(axis_name)
    bits = exchange_bits(size)
    pending = [keep]
    for bit in range(bits):
        if bit > 0:
            split = pending[0].shape[0] // 2
            send = sum(part[split:] for part in pending[1:])
            send = (pending[0][split:] + send).astype(jnp.bfloat16)
            pending = [part[:split] for part in pending]
        pending.append(swap_with(send, axis_name, size, bit).astype(jnp.float32))
    return sum(pending[1:], pending[0])


def contract_rows(left, right):
    return lax.dot_general(
        left, right, (((0,), (0,)), ((), ())), preferred_element_type=jnp.float32
    )


def contract_cols(left, right):
    return lax.dot_general(
        left, right, (((1,), (1,)), ((), ())), preferred_element_type=jnp.float32
    )


def stacked_heads(ref, c):
    return jnp.concatenate(
        [
            ref[:, h * HEAD_SIZE:(h + 1) * HEAD_SIZE]
            for h in range(c * GROUP_HEADS, (c + 1) * GROUP_HEADS)
        ],
        axis=0,
    )


def own_stats_kernel(q_ref, do_ref, ks_ref, vs_ref, self_ref, stats_ref):
    score_scale = HEAD_SIZE ** (-0.5)
    self_seen = jnp.concatenate([self_ref[...]] * GROUP_HEADS, axis=1) > 0.5
    for c in range(KEY_HEADS):
        columns = slice(c * HEAD_SIZE, (c + 1) * HEAD_SIZE)
        q = stacked_heads(q_ref, c)
        do = stacked_heads(do_ref, c)
        ss = jnp.where(self_seen, contract_cols(ks_ref[:, columns], q) * score_scale, masked_score)
        top = jnp.max(ss, axis=0, keepdims=True)
        es = jnp.exp(ss - top)
        gs = contract_cols(vs_ref[:, columns], do)
        stats_ref[c:c + 1, :] = top
        stats_ref[KEY_HEADS + c:KEY_HEADS + c + 1, :] = jnp.sum(es, axis=0, keepdims=True)
        stats_ref[2 * KEY_HEADS + c:2 * KEY_HEADS + c + 1, :] = jnp.sum(
            es * gs, axis=0, keepdims=True
        )


def document_kernel(
    q_ref, do_ref, kva_ref, kvb_ref, vis_ref, own_ref, live_ref,
    keep_ref, send_ref, stats_ref, dsd_ref,
):
    width = KEY_HEADS * HEAD_SIZE
    half = kva_ref.shape[0]
    score_scale = HEAD_SIZE ** (-0.5)
    doc_seen = jnp.concatenate([vis_ref[...]] * GROUP_HEADS, axis=1) > 0.5
    live = jnp.concatenate([live_ref[...]] * GROUP_HEADS, axis=1)
    for c in range(KEY_HEADS):
        columns = slice(c * HEAD_SIZE, (c + 1) * HEAD_SIZE)
        value_columns = slice(width + c * HEAD_SIZE, width + (c + 1) * HEAD_SIZE)
        kd = jnp.concatenate([kva_ref[:, columns], kvb_ref[:, columns]], axis=0)
        vd = jnp.concatenate([kva_ref[:, value_columns], kvb_ref[:, value_columns]], axis=0)
        q = stacked_heads(q_ref, c)
        do = stacked_heads(do_ref, c)
        own_top = own_ref[c:c + 1, :]
        own_total = own_ref[KEY_HEADS + c:KEY_HEADS + c + 1, :]
        own_weighted = own_ref[2 * KEY_HEADS + c:2 * KEY_HEADS + c + 1, :]
        sd = jnp.where(doc_seen, contract_cols(kd, q) * score_scale, masked_score)
        top = jnp.maximum(jnp.max(sd, axis=0, keepdims=True), own_top)
        ed = jnp.exp(sd - top)
        factor = jnp.exp(own_top - top)
        gd = contract_cols(vd, do)
        total = jnp.sum(ed, axis=0, keepdims=True) + own_total * factor
        weight = live / total
        drift = (jnp.sum(ed * gd, axis=0, keepdims=True) + own_weighted * factor) * weight
        pd = ed * weight
        dsd = (pd * (gd - drift)).astype(jnp.bfloat16)
        dsd_ref[c] = dsd
        stats_ref[c:c + 1, :] = top
        stats_ref[KEY_HEADS + c:KEY_HEADS + c + 1, :] = weight
        stats_ref[2 * KEY_HEADS + c:2 * KEY_HEADS + c + 1, :] = drift
        doc_key = jnp.dot(dsd, q, preferred_element_type=jnp.float32) * score_scale
        doc_value = jnp.dot(pd.astype(jnp.bfloat16), do, preferred_element_type=jnp.float32)
        keep_ref[:, columns] = doc_key[:half]
        send_ref[:, columns] = doc_key[half:].astype(send_ref.dtype)
        keep_ref[:, value_columns] = doc_value[:half]
        send_ref[:, value_columns] = doc_value[half:].astype(send_ref.dtype)


def response_kernel(
    q_ref, do_ref, kva_ref, kvb_ref, ks_ref, vs_ref, self_ref, stats_ref, dsd_ref,
    dq_ref, sk_ref, sv_ref,
):
    token_rows = q_ref.shape[0]
    score_scale = HEAD_SIZE ** (-0.5)
    self_seen = jnp.concatenate([self_ref[...]] * GROUP_HEADS, axis=1) > 0.5
    for c in range(KEY_HEADS):
        columns = slice(c * HEAD_SIZE, (c + 1) * HEAD_SIZE)
        kd = jnp.concatenate([kva_ref[:, columns], kvb_ref[:, columns]], axis=0)
        ks = ks_ref[:, columns]
        q = stacked_heads(q_ref, c)
        do = stacked_heads(do_ref, c)
        top = stats_ref[c:c + 1, :]
        weight = stats_ref[KEY_HEADS + c:KEY_HEADS + c + 1, :]
        drift = stats_ref[2 * KEY_HEADS + c:2 * KEY_HEADS + c + 1, :]
        ss = jnp.where(self_seen, contract_cols(ks, q) * score_scale, masked_score)
        ps = jnp.exp(ss - top) * weight
        gs = contract_cols(vs_ref[:, columns], do)
        dss = (ps * (gs - drift)).astype(jnp.bfloat16)
        dq = (contract_rows(dsd_ref[c], kd) + contract_rows(dss, ks)) * score_scale
        for g in range(GROUP_HEADS):
            h = c * GROUP_HEADS + g
            dq_ref[:, h * HEAD_SIZE:(h + 1) * HEAD_SIZE] = dq[
                g * token_rows:(g + 1) * token_rows
            ].astype(dq_ref.dtype)
        sk_ref[:, columns] = (
            jnp.dot(dss, q, preferred_element_type=jnp.float32) * score_scale
        ).astype(sk_ref.dtype)
        sv_ref[:, columns] = jnp.dot(
            ps.astype(jnp.bfloat16), do, preferred_element_type=jnp.float32
        ).astype(sv_ref.dtype)


def per_device(
    queries,
    response_keys,
    response_values,
    document_keys,
    document_values,
    grad_out,
    lengths,
    doc_mask,
):
    token_rows = queries.shape[0]
    responses_here = lengths.shape[0]
    resp_len = token_rows // responses_here
    mask_blocks = doc_mask.shape[1]
    key_value_width = KEY_HEADS * HEAD_SIZE
    positions = jnp.arange(token_rows, dtype=jnp.int32)
    owners = positions // resp_len
    within = positions % resp_len
    live = (within < jnp.repeat(lengths, resp_len)).astype(jnp.float32)[None, :]
    spots = np.arange(token_rows)
    holders_here = spots // resp_len
    self_visible = jnp.asarray(
        (holders_here[:, None] == holders_here[None, :]) & (spots[:, None] <= spots[None, :]),
        jnp.float32,
    )
    size = lax.axis_size("resp")
    doc_mine, doc_other = gather_rows(
        jnp.concatenate([document_keys, document_values], axis=1), "resp"
    )
    slab_rows = document_keys.shape[0]
    doc_rows = size * slab_rows
    half_rows = doc_rows // 2
    block_rows = doc_rows // mask_blocks
    holders = jnp.bitwise_xor(
        lax.axis_index("resp"), jnp.asarray(np.repeat(exchange_pattern(size), slab_rows), jnp.int32)
    )
    global_rows = holders * slab_rows + jnp.asarray(np.tile(np.arange(slab_rows), size), jnp.int32)
    row_masks = jnp.repeat(doc_mask, resp_len, axis=0)
    doc_visible = (jnp.take(row_masks.T, global_rows // block_rows, axis=0) == 1).astype(
        jnp.float32
    )
    stacked_rows = GROUP_HEADS * token_rows
    own_stats = pl.pallas_call(
        own_stats_kernel,
        out_shape=jax.ShapeDtypeStruct((3 * KEY_HEADS, stacked_rows), jnp.float32),
    )(queries, grad_out, response_keys, response_values, self_visible)
    doc_keep, doc_send, row_stats, doc_dscore = pl.pallas_call(
        document_kernel,
        out_shape=(
            jax.ShapeDtypeStruct((half_rows, 2 * key_value_width), jnp.float32),
            jax.ShapeDtypeStruct((half_rows, 2 * key_value_width), jnp.bfloat16),
            jax.ShapeDtypeStruct((3 * KEY_HEADS, stacked_rows), jnp.float32),
            jax.ShapeDtypeStruct((KEY_HEADS, doc_rows, stacked_rows), jnp.bfloat16),
        ),
    )(queries, grad_out, doc_mine, doc_other, doc_visible, own_stats, live)
    query_gradient, self_key, self_value = pl.pallas_call(
        response_kernel,
        out_shape=(
            jax.ShapeDtypeStruct(queries.shape, jnp.bfloat16),
            jax.ShapeDtypeStruct(response_keys.shape, jnp.bfloat16),
            jax.ShapeDtypeStruct(response_values.shape, jnp.bfloat16),
        ),
    )(
        queries, grad_out, doc_mine, doc_other, response_keys, response_values,
        self_visible, row_stats, doc_dscore,
    )
    summed = scatter_sum_rows(doc_keep, doc_send, "resp")
    return (
        query_gradient,
        summed[:, :key_value_width].astype(jnp.bfloat16),
        summed[:, key_value_width:].astype(jnp.bfloat16),
        self_key,
        self_value,
    )


def solution(mesh):
    return jax.shard_map(
        per_device,
        mesh=mesh,
        in_specs=(
            P(("grp", "resp"), None),
            P(("grp", "resp"), None),
            P(("grp", "resp"), None),
            P(("grp", "resp"), None),
            P(("grp", "resp"), None),
            P(("grp", "resp"), None),
            P(("grp", "resp")),
            P(("grp", "resp"), None),
        ),
        out_specs=(
            P(("grp", "resp"), None),
            P(("grp", "resp"), None),
            P(("grp", "resp"), None),
            P(("grp", "resp"), None),
            P(("grp", "resp"), None),
        ),
        check_vma=False,
    )
```

```python
import jax
import numpy as np
import jax.numpy as jnp
from jax import lax
from jax.experimental import pallas as pl
from jax.experimental.pallas import tpu as pltpu
from jax.sharding import PartitionSpec as P

KEY_HEADS = 4
GROUP_HEADS = 5
HEAD_SIZE = 128


masked_score = -1e30


def exchange_bits(size):
    bits = size.bit_length() - 1
    if (1 << bits) != size:
        return None
    return bits


def swap_with(block, axis_name, size, bit):
    pairs = [(index, index ^ (1 << bit)) for index in range(size)]
    return lax.ppermute(block, axis_name, pairs)


def exchange_pattern(size):
    bits = exchange_bits(size)
    return [int(format(spot, "0%db" % bits)[::-1], 2) for spot in range(size)]


def gather_rows(blocks, axis_name):
    size = lax.axis_size(axis_name)
    bits = exchange_bits(size)
    halves = None
    for bit in reversed(range(bits)):
        if halves is not None:
            blocks = jnp.concatenate(halves)
        halves = (blocks, swap_with(blocks, axis_name, size, bit))
    return halves


def scatter_sum_rows(keep, send, axis_name):
    size = lax.axis_size(axis_name)
    bits = exchange_bits(size)
    pending = [keep]
    for bit in range(bits):
        if bit > 0:
            split = pending[0].shape[0] // 2
            send = sum(part[split:] for part in pending[1:])
            send = (pending[0][split:] + send).astype(jnp.bfloat16)
            pending = [part[:split] for part in pending]
        pending.append(swap_with(send, axis_name, size, bit).astype(jnp.float32))
    return sum(pending[1:], pending[0])


def contract_rows(left, right):
    return lax.dot_general(
        left, right, (((0,), (0,)), ((), ())), preferred_element_type=jnp.float32
    )


def contract_cols(left, right):
    return lax.dot_general(
        left, right, (((1,), (1,)), ((), ())), preferred_element_type=jnp.float32
    )


def stacked_heads(ref, c):
    return jnp.concatenate(
        [
            ref[:, h * HEAD_SIZE:(h + 1) * HEAD_SIZE]
            for h in range(c * GROUP_HEADS, (c + 1) * GROUP_HEADS)
        ],
        axis=0,
    )


def attention_kernel(
    q_hbm, do_hbm, kva_ref, kvb_ref, ks_ref, vs_ref, vis_ref, self_ref, live_ref,
    dq_ref, keep_ref, send_ref, sk_ref, sv_ref, q_buf, do_buf, arrivals,
):
    token_rows = q_buf.shape[1]
    head_block = GROUP_HEADS * HEAD_SIZE

    def fetch(c, slot):
        block = slice(c * head_block, (c + 1) * head_block)
        return (
            pltpu.make_async_copy(q_hbm.at[:, block], q_buf.at[slot], arrivals.at[0, slot]),
            pltpu.make_async_copy(do_hbm.at[:, block], do_buf.at[slot], arrivals.at[1, slot]),
        )

    pending = fetch(0, 0)
    for copy in pending:
        copy.start()
    width = KEY_HEADS * HEAD_SIZE
    half = kva_ref.shape[0]
    doc_rows = 2 * half
    score_scale = HEAD_SIZE ** (-0.5)
    seen = jnp.concatenate(
        [jnp.concatenate([vis_ref[...], self_ref[...]], axis=0)] * GROUP_HEADS, axis=1
    ) > 0.5
    live = jnp.concatenate([live_ref[...]] * GROUP_HEADS, axis=1)
    for c in range(KEY_HEADS):
        slot = c % 2
        current = pending
        if c + 1 < KEY_HEADS:
            pending = fetch(c + 1, 1 - slot)
            for copy in pending:
                copy.start()
        for copy in current:
            copy.wait()
        columns = slice(c * HEAD_SIZE, (c + 1) * HEAD_SIZE)
        value_columns = slice(width + c * HEAD_SIZE, width + (c + 1) * HEAD_SIZE)
        keys = jnp.concatenate(
            [kva_ref[:, columns], kvb_ref[:, columns], ks_ref[:, columns]], axis=0
        )
        values = jnp.concatenate(
            [kva_ref[:, value_columns], kvb_ref[:, value_columns], vs_ref[:, columns]], axis=0
        )
        q = stacked_heads(q_buf.at[slot], 0)
        do = stacked_heads(do_buf.at[slot], 0)
        score = jnp.where(seen, contract_cols(keys, q) * score_scale, masked_score)
        top = jnp.max(score, axis=0, keepdims=True)
        grown = jnp.exp(score - top)
        prob = grown * (live / jnp.sum(grown, axis=0, keepdims=True))
        slope = contract_cols(values, do)
        drift = jnp.sum(prob * slope, axis=0, keepdims=True)
        dscore = (prob * (slope - drift)).astype(jnp.bfloat16)
        dq = contract_rows(dscore, keys) * score_scale
        for g in range(GROUP_HEADS):
            h = c * GROUP_HEADS + g
            dq_ref[:, h * HEAD_SIZE:(h + 1) * HEAD_SIZE] = dq[
                g * token_rows:(g + 1) * token_rows
            ].astype(dq_ref.dtype)
        key_total = jnp.dot(dscore, q, preferred_element_type=jnp.float32) * score_scale
        value_total = jnp.dot(prob.astype(jnp.bfloat16), do, preferred_element_type=jnp.float32)
        keep_ref[:, columns] = key_total[:half]
        send_ref[:, columns] = key_total[half:doc_rows].astype(send_ref.dtype)
        keep_ref[:, value_columns] = value_total[:half]
        send_ref[:, value_columns] = value_total[half:doc_rows].astype(send_ref.dtype)
        sk_ref[:, columns] = key_total[doc_rows:].astype(sk_ref.dtype)
        sv_ref[:, columns] = value_total[doc_rows:].astype(sv_ref.dtype)


def per_device(
    queries,
    response_keys,
    response_values,
    document_keys,
    document_values,
    grad_out,
    lengths,
    doc_mask,
):
    token_rows = queries.shape[0]
    responses_here = lengths.shape[0]
    resp_len = token_rows // responses_here
    mask_blocks = doc_mask.shape[1]
    key_value_width = KEY_HEADS * HEAD_SIZE
    positions = jnp.arange(token_rows, dtype=jnp.int32)
    owners = positions // resp_len
    within = positions % resp_len
    live = (within < jnp.repeat(lengths, resp_len)).astype(jnp.float32)[None, :]
    spots = np.arange(token_rows)
    holders_here = spots // resp_len
    self_visible = jnp.asarray(
        (holders_here[:, None] == holders_here[None, :]) & (spots[:, None] <= spots[None, :]),
        jnp.float32,
    )
    size = lax.axis_size("resp")
    doc_mine, doc_other = gather_rows(
        jnp.concatenate([document_keys, document_values], axis=1), "resp"
    )
    slab_rows = document_keys.shape[0]
    doc_rows = size * slab_rows
    half_rows = doc_rows // 2
    block_rows = doc_rows // mask_blocks
    holders = jnp.bitwise_xor(
        lax.axis_index("resp"), jnp.asarray(np.repeat(exchange_pattern(size), slab_rows), jnp.int32)
    )
    global_rows = holders * slab_rows + jnp.asarray(np.tile(np.arange(slab_rows), size), jnp.int32)
    row_masks = jnp.repeat(doc_mask, resp_len, axis=0)
    doc_visible = (jnp.take(row_masks.T, global_rows // block_rows, axis=0) == 1).astype(
        jnp.float32
    )
    query_gradient, doc_keep, doc_send, self_key, self_value = pl.pallas_call(
        attention_kernel,
        out_shape=(
            jax.ShapeDtypeStruct(queries.shape, jnp.bfloat16),
            jax.ShapeDtypeStruct((half_rows, 2 * key_value_width), jnp.float32),
            jax.ShapeDtypeStruct((half_rows, 2 * key_value_width), jnp.bfloat16),
            jax.ShapeDtypeStruct(response_keys.shape, jnp.bfloat16),
            jax.ShapeDtypeStruct(response_values.shape, jnp.bfloat16),
        ),
        in_specs=[pl.BlockSpec(memory_space=pl.ANY)] * 2
        + [pl.BlockSpec(memory_space=pltpu.VMEM)] * 7,
        scratch_shapes=[
            pltpu.VMEM((2, token_rows, GROUP_HEADS * HEAD_SIZE), jnp.bfloat16),
            pltpu.VMEM((2, token_rows, GROUP_HEADS * HEAD_SIZE), jnp.bfloat16),
            pltpu.SemaphoreType.DMA((2, 2)),
        ],
    )(
        queries,
        grad_out,
        doc_mine,
        doc_other,
        response_keys,
        response_values,
        doc_visible,
        self_visible,
        live,
    )
    summed = scatter_sum_rows(doc_keep, doc_send, "resp")
    return (
        query_gradient,
        summed[:, :key_value_width].astype(jnp.bfloat16),
        summed[:, key_value_width:].astype(jnp.bfloat16),
        self_key,
        self_value,
    )


def solution(mesh):
    return jax.shard_map(
        per_device,
        mesh=mesh,
        in_specs=(
            P(("grp", "resp"), None),
            P(("grp", "resp"), None),
            P(("grp", "resp"), None),
            P(("grp", "resp"), None),
            P(("grp", "resp"), None),
            P(("grp", "resp"), None),
            P(("grp", "resp")),
            P(("grp", "resp"), None),
        ),
        out_specs=(
            P(("grp", "resp"), None),
            P(("grp", "resp"), None),
            P(("grp", "resp"), None),
            P(("grp", "resp"), None),
            P(("grp", "resp"), None),
        ),
        check_vma=False,
    )
```

```python
import jax
import numpy as np
import jax.numpy as jnp
from jax import lax
from jax.experimental import pallas as pl
from jax.sharding import PartitionSpec as P

KEY_HEADS = 4
GROUP_HEADS = 5
HEAD_SIZE = 128


masked_score = -1e30


def exchange_bits(size):
    bits = size.bit_length() - 1
    if (1 << bits) != size:
        return None
    return bits


def swap_with(block, axis_name, size, bit):
    pairs = [(index, index ^ (1 << bit)) for index in range(size)]
    return lax.ppermute(block, axis_name, pairs)


def exchange_sequence(bits):
    order = list(reversed(range(bits)))
    if bits >= 3:
        order[-3], order[-2] = order[-2], order[-3]
    return order


def exchange_pattern(size):
    order = exchange_sequence(exchange_bits(size))
    return [
        sum(((spot >> step) & 1) << bit for step, bit in enumerate(order)) for spot in range(size)
    ]


def gather_rows(blocks, axis_name):
    size = lax.axis_size(axis_name)
    bits = exchange_bits(size)
    halves = None
    for bit in exchange_sequence(bits):
        if halves is not None:
            blocks = jnp.concatenate(halves)
        halves = (blocks, swap_with(blocks, axis_name, size, bit))
    return halves


def scatter_sum_rows(keep, send, axis_name):
    size = lax.axis_size(axis_name)
    bits = exchange_bits(size)
    pending = [keep]
    for step, bit in enumerate(reversed(exchange_sequence(bits))):
        if step > 0:
            split = pending[0].shape[0] // 2
            send = sum(part[split:] for part in pending[1:])
            send = (pending[0][split:] + send).astype(jnp.bfloat16)
            pending = [part[:split] for part in pending]
        pending.append(swap_with(send, axis_name, size, bit).astype(jnp.float32))
    return sum(pending[1:], pending[0])


def contract_rows(left, right):
    return lax.dot_general(
        left, right, (((0,), (0,)), ((), ())), preferred_element_type=jnp.float32
    )


def contract_cols(left, right):
    return lax.dot_general(
        left, right, (((1,), (1,)), ((), ())), preferred_element_type=jnp.float32
    )


def stacked_heads(ref, c):
    return jnp.concatenate(
        [
            ref[:, h * HEAD_SIZE:(h + 1) * HEAD_SIZE]
            for h in range(c * GROUP_HEADS, (c + 1) * GROUP_HEADS)
        ],
        axis=0,
    )


def attention_kernel(
    q_ref, do_ref, kva_ref, kvb_ref, ks_ref, vs_ref, vis_ref, self_ref, live_ref,
    dq_ref, keep_ref, send_ref, sk_ref, sv_ref,
):
    token_rows = q_ref.shape[0]
    width = KEY_HEADS * HEAD_SIZE
    half = kva_ref.shape[0]
    doc_rows = 2 * half
    score_scale = HEAD_SIZE ** (-0.5)
    seen = jnp.concatenate(
        [jnp.concatenate([vis_ref[...], self_ref[...]], axis=0)] * GROUP_HEADS, axis=1
    ) > 0.5
    live = jnp.concatenate([live_ref[...]] * GROUP_HEADS, axis=1)
    for c in range(KEY_HEADS):
        columns = slice(c * HEAD_SIZE, (c + 1) * HEAD_SIZE)
        value_columns = slice(width + c * HEAD_SIZE, width + (c + 1) * HEAD_SIZE)
        keys = jnp.concatenate(
            [kva_ref[:, columns], kvb_ref[:, columns], ks_ref[:, columns]], axis=0
        )
        values = jnp.concatenate(
            [kva_ref[:, value_columns], kvb_ref[:, value_columns], vs_ref[:, columns]], axis=0
        )
        q = stacked_heads(q_ref, c)
        do = stacked_heads(do_ref, c)
        score = jnp.where(seen, contract_cols(keys, q) * score_scale, masked_score)
        top = jnp.max(score, axis=0, keepdims=True)
        grown = jnp.exp(score - top)
        prob = grown * (live / jnp.sum(grown, axis=0, keepdims=True))
        slope = contract_cols(values, do)
        drift = jnp.sum(prob * slope, axis=0, keepdims=True)
        dscore = (prob * (slope - drift)).astype(jnp.bfloat16)
        dq = contract_rows(dscore, keys) * score_scale
        for g in range(GROUP_HEADS):
            h = c * GROUP_HEADS + g
            dq_ref[:, h * HEAD_SIZE:(h + 1) * HEAD_SIZE] = dq[
                g * token_rows:(g + 1) * token_rows
            ].astype(dq_ref.dtype)
        key_total = jnp.dot(dscore, q, preferred_element_type=jnp.float32) * score_scale
        value_total = jnp.dot(prob.astype(jnp.bfloat16), do, preferred_element_type=jnp.float32)
        keep_ref[:, columns] = key_total[:half]
        send_ref[:, columns] = key_total[half:doc_rows].astype(send_ref.dtype)
        keep_ref[:, value_columns] = value_total[:half]
        send_ref[:, value_columns] = value_total[half:doc_rows].astype(send_ref.dtype)
        sk_ref[:, columns] = key_total[doc_rows:].astype(sk_ref.dtype)
        sv_ref[:, columns] = value_total[doc_rows:].astype(sv_ref.dtype)


def per_device(
    queries,
    response_keys,
    response_values,
    document_keys,
    document_values,
    grad_out,
    lengths,
    doc_mask,
):
    token_rows = queries.shape[0]
    responses_here = lengths.shape[0]
    resp_len = token_rows // responses_here
    mask_blocks = doc_mask.shape[1]
    key_value_width = KEY_HEADS * HEAD_SIZE
    positions = jnp.arange(token_rows, dtype=jnp.int32)
    owners = positions // resp_len
    within = positions % resp_len
    live = (within < jnp.repeat(lengths, resp_len)).astype(jnp.float32)[None, :]
    spots = np.arange(token_rows)
    holders_here = spots // resp_len
    self_visible = jnp.asarray(
        (holders_here[:, None] == holders_here[None, :]) & (spots[:, None] <= spots[None, :]),
        jnp.float32,
    )
    size = lax.axis_size("resp")
    doc_mine, doc_other = gather_rows(
        jnp.concatenate([document_keys, document_values], axis=1), "resp"
    )
    slab_rows = document_keys.shape[0]
    doc_rows = size * slab_rows
    half_rows = doc_rows // 2
    block_rows = doc_rows // mask_blocks
    holders = jnp.bitwise_xor(
        lax.axis_index("resp"), jnp.asarray(np.repeat(exchange_pattern(size), slab_rows), jnp.int32)
    )
    global_rows = holders * slab_rows + jnp.asarray(np.tile(np.arange(slab_rows), size), jnp.int32)
    row_masks = jnp.repeat(doc_mask, resp_len, axis=0)
    doc_visible = (jnp.take(row_masks.T, global_rows // block_rows, axis=0) == 1).astype(
        jnp.float32
    )
    query_gradient, doc_keep, doc_send, self_key, self_value = pl.pallas_call(
        attention_kernel,
        out_shape=(
            jax.ShapeDtypeStruct(queries.shape, jnp.bfloat16),
            jax.ShapeDtypeStruct((half_rows, 2 * key_value_width), jnp.float32),
            jax.ShapeDtypeStruct((half_rows, 2 * key_value_width), jnp.bfloat16),
            jax.ShapeDtypeStruct(response_keys.shape, jnp.bfloat16),
            jax.ShapeDtypeStruct(response_values.shape, jnp.bfloat16),
        ),
    )(
        queries,
        grad_out,
        doc_mine,
        doc_other,
        response_keys,
        response_values,
        doc_visible,
        self_visible,
        live,
    )
    summed = scatter_sum_rows(doc_keep, doc_send, "resp")
    return (
        query_gradient,
        summed[:, :key_value_width].astype(jnp.bfloat16),
        summed[:, key_value_width:].astype(jnp.bfloat16),
        self_key,
        self_value,
    )


def solution(mesh):
    return jax.shard_map(
        per_device,
        mesh=mesh,
        in_specs=(
            P(("grp", "resp"), None),
            P(("grp", "resp"), None),
            P(("grp", "resp"), None),
            P(("grp", "resp"), None),
            P(("grp", "resp"), None),
            P(("grp", "resp"), None),
            P(("grp", "resp")),
            P(("grp", "resp"), None),
        ),
        out_specs=(
            P(("grp", "resp"), None),
            P(("grp", "resp"), None),
            P(("grp", "resp"), None),
            P(("grp", "resp"), None),
            P(("grp", "resp"), None),
        ),
        check_vma=False,
    )
```

```python
import jax
import numpy as np
import jax.numpy as jnp
from jax import lax
from jax.experimental import pallas as pl
from jax.sharding import PartitionSpec as P

KEY_HEADS = 4
GROUP_HEADS = 5
HEAD_SIZE = 128


masked_score = -1e30


def exchange_bits(size):
    bits = size.bit_length() - 1
    if (1 << bits) != size:
        return None
    return bits


def swap_with(block, axis_name, size, bit):
    pairs = [(index, index ^ (1 << bit)) for index in range(size)]
    return lax.ppermute(block, axis_name, pairs)


def exchange_sequence(bits):
    order = list(reversed(range(bits)))
    if bits >= 3:
        order[-3], order[-2] = order[-2], order[-3]
    return order


def exchange_pattern(size):
    order = exchange_sequence(exchange_bits(size))
    return [
        sum(((spot >> step) & 1) << bit for step, bit in enumerate(order)) for spot in range(size)
    ]


def gather_rows(blocks, axis_name):
    size = lax.axis_size(axis_name)
    bits = exchange_bits(size)
    halves = None
    for bit in exchange_sequence(bits):
        if halves is not None:
            blocks = jnp.concatenate(
                [jnp.concatenate(part, axis=1) if isinstance(part, tuple) else part for part in halves]
            )
        halves = (blocks, swap_with(blocks, axis_name, size, bit))
    return halves


def scatter_sum_rows(keep, send, axis_name):
    size = lax.axis_size(axis_name)
    bits = exchange_bits(size)
    pending = [keep]
    for step, bit in enumerate(reversed(exchange_sequence(bits))):
        if step > 0:
            split = pending[0].shape[0] // 2
            send = sum(part[split:] for part in pending[1:])
            send = (pending[0][split:] + send).astype(jnp.bfloat16)
            pending = [part[:split] for part in pending]
        pending.append(swap_with(send, axis_name, size, bit).astype(jnp.float32))
    return sum(pending[1:], pending[0])


def contract_rows(left, right):
    return lax.dot_general(
        left, right, (((0,), (0,)), ((), ())), preferred_element_type=jnp.float32
    )


def contract_cols(left, right):
    return lax.dot_general(
        left, right, (((1,), (1,)), ((), ())), preferred_element_type=jnp.float32
    )


def stacked_heads(ref, c):
    return jnp.concatenate(
        [
            ref[:, h * HEAD_SIZE:(h + 1) * HEAD_SIZE]
            for h in range(c * GROUP_HEADS, (c + 1) * GROUP_HEADS)
        ],
        axis=0,
    )


def attention_kernel(
    q_ref, do_ref, kva_ref, kvb_ref, ks_ref, vs_ref, vis_ref, self_ref, live_ref,
    dq_ref, keep_ref, send_ref, sk_ref, sv_ref,
):
    token_rows = q_ref.shape[0]
    width = KEY_HEADS * HEAD_SIZE
    half = kva_ref.shape[0]
    doc_rows = 2 * half
    score_scale = HEAD_SIZE ** (-0.5)
    seen = jnp.concatenate(
        [jnp.concatenate([vis_ref[...], self_ref[...]], axis=0)] * GROUP_HEADS, axis=1
    ) > 0.5
    live = jnp.concatenate([live_ref[...]] * GROUP_HEADS, axis=1)
    for c in range(KEY_HEADS):
        columns = slice(c * HEAD_SIZE, (c + 1) * HEAD_SIZE)
        value_columns = slice(width + c * HEAD_SIZE, width + (c + 1) * HEAD_SIZE)
        keys = jnp.concatenate(
            [kva_ref[:, columns], kvb_ref[:, columns], ks_ref[:, columns]], axis=0
        )
        values = jnp.concatenate(
            [kva_ref[:, value_columns], kvb_ref[:, value_columns], vs_ref[:, columns]], axis=0
        )
        q = stacked_heads(q_ref, c)
        do = stacked_heads(do_ref, c)
        score = jnp.where(seen, contract_cols(keys, q) * score_scale, masked_score)
        top = jnp.max(score, axis=0, keepdims=True)
        grown = jnp.exp(score - top)
        prob = grown * (live / jnp.sum(grown, axis=0, keepdims=True))
        slope = contract_cols(values, do)
        drift = jnp.sum(prob * slope, axis=0, keepdims=True)
        dscore = (prob * (slope - drift)).astype(jnp.bfloat16)
        dq = contract_rows(dscore, keys) * score_scale
        for g in range(GROUP_HEADS):
            h = c * GROUP_HEADS + g
            dq_ref[:, h * HEAD_SIZE:(h + 1) * HEAD_SIZE] = dq[
                g * token_rows:(g + 1) * token_rows
            ].astype(dq_ref.dtype)
        key_total = jnp.dot(dscore, q, preferred_element_type=jnp.float32) * score_scale
        value_total = jnp.dot(prob.astype(jnp.bfloat16), do, preferred_element_type=jnp.float32)
        keep_ref[:, columns] = key_total[:half]
        send_ref[:, columns] = key_total[half:doc_rows].astype(send_ref.dtype)
        keep_ref[:, value_columns] = value_total[:half]
        send_ref[:, value_columns] = value_total[half:doc_rows].astype(send_ref.dtype)
        sk_ref[:, columns] = key_total[doc_rows:].astype(sk_ref.dtype)
        sv_ref[:, columns] = value_total[doc_rows:].astype(sv_ref.dtype)


def per_device(
    queries,
    response_keys,
    response_values,
    document_keys,
    document_values,
    grad_out,
    lengths,
    doc_mask,
):
    token_rows = queries.shape[0]
    responses_here = lengths.shape[0]
    resp_len = token_rows // responses_here
    mask_blocks = doc_mask.shape[1]
    key_value_width = KEY_HEADS * HEAD_SIZE
    positions = jnp.arange(token_rows, dtype=jnp.int32)
    owners = positions // resp_len
    within = positions % resp_len
    live = (within < jnp.repeat(lengths, resp_len)).astype(jnp.float32)[None, :]
    spots = np.arange(token_rows)
    holders_here = spots // resp_len
    self_visible = jnp.asarray(
        (holders_here[:, None] == holders_here[None, :]) & (spots[:, None] <= spots[None, :]),
        jnp.float32,
    )
    size = lax.axis_size("resp")
    doc_mine, doc_other = gather_rows((document_keys, document_values), "resp")
    slab_rows = document_keys.shape[0]
    doc_rows = size * slab_rows
    half_rows = doc_rows // 2
    block_rows = doc_rows // mask_blocks
    holders = jnp.bitwise_xor(
        lax.axis_index("resp"), jnp.asarray(np.repeat(exchange_pattern(size), slab_rows), jnp.int32)
    )
    global_rows = holders * slab_rows + jnp.asarray(np.tile(np.arange(slab_rows), size), jnp.int32)
    row_masks = jnp.repeat(doc_mask, resp_len, axis=0)
    doc_visible = (jnp.take(row_masks.T, global_rows // block_rows, axis=0) == 1).astype(
        jnp.float32
    )
    query_gradient, doc_keep, doc_send, self_key, self_value = pl.pallas_call(
        attention_kernel,
        out_shape=(
            jax.ShapeDtypeStruct(queries.shape, jnp.bfloat16),
            jax.ShapeDtypeStruct((half_rows, 2 * key_value_width), jnp.float32),
            jax.ShapeDtypeStruct((half_rows, 2 * key_value_width), jnp.bfloat16),
            jax.ShapeDtypeStruct(response_keys.shape, jnp.bfloat16),
            jax.ShapeDtypeStruct(response_values.shape, jnp.bfloat16),
        ),
    )(
        queries,
        grad_out,
        doc_mine,
        doc_other,
        response_keys,
        response_values,
        doc_visible,
        self_visible,
        live,
    )
    summed = scatter_sum_rows(doc_keep, doc_send, "resp")
    return (
        query_gradient,
        summed[:, :key_value_width].astype(jnp.bfloat16),
        summed[:, key_value_width:].astype(jnp.bfloat16),
        self_key,
        self_value,
    )


def solution(mesh):
    return jax.shard_map(
        per_device,
        mesh=mesh,
        in_specs=(
            P(("grp", "resp"), None),
            P(("grp", "resp"), None),
            P(("grp", "resp"), None),
            P(("grp", "resp"), None),
            P(("grp", "resp"), None),
            P(("grp", "resp"), None),
            P(("grp", "resp")),
            P(("grp", "resp"), None),
        ),
        out_specs=(
            P(("grp", "resp"), None),
            P(("grp", "resp"), None),
            P(("grp", "resp"), None),
            P(("grp", "resp"), None),
            P(("grp", "resp"), None),
        ),
        check_vma=False,
    )
```

```python
import jax
import numpy as np
import jax.numpy as jnp
from jax import lax
from jax.experimental import pallas as pl
from jax.sharding import PartitionSpec as P

KEY_HEADS = 4
GROUP_HEADS = 5
HEAD_SIZE = 128


masked_score = -1e30


def exchange_bits(size):
    bits = size.bit_length() - 1
    if (1 << bits) != size:
        return None
    return bits


def swap_with(block, axis_name, size, bit):
    pairs = [(index, index ^ (1 << bit)) for index in range(size)]
    return lax.ppermute(block, axis_name, pairs)


def exchange_pattern(size):
    bits = exchange_bits(size)
    return [int(format(spot, "0%db" % bits)[::-1], 2) for spot in range(size)]


def gather_rows(blocks, axis_name):
    size = lax.axis_size(axis_name)
    bits = exchange_bits(size)
    halves = None
    for bit in reversed(range(bits)):
        if halves is not None:
            blocks = jnp.concatenate(halves)
        halves = (blocks, swap_with(blocks, axis_name, size, bit))
    return halves


def scatter_sum_rows(keep, send, axis_name):
    size = lax.axis_size(axis_name)
    bits = exchange_bits(size)
    pending = [keep]
    ring_bits = bits - 2 if bits >= 3 else bits
    for bit in range(ring_bits):
        if bit > 0:
            split = pending[0].shape[0] // 2
            send = sum(part[split:] for part in pending[1:])
            send = (pending[0][split:] + send).astype(jnp.bfloat16)
            pending = [part[:split] for part in pending]
        pending.append(swap_with(send, axis_name, size, bit).astype(jnp.float32))
    if ring_bits == bits:
        return sum(pending[1:], pending[0])
    if ring_bits == 0:
        pending = [keep, send]
    quarter = pending[0].shape[0] // 4
    received = []
    for spot in range(1, 4):
        rows = slice(spot * quarter, (spot + 1) * quarter)
        piece = sum(part[rows] for part in pending[1:])
        piece = (pending[0][rows] + piece).astype(jnp.bfloat16)
        flip = ((spot >> 1) & 1) << (bits - 2) | (spot & 1) << (bits - 1)
        pairs = [(index, index ^ flip) for index in range(size)]
        received.append(lax.ppermute(piece, axis_name, pairs).astype(jnp.float32))
    total = sum(part[:quarter] for part in pending[1:])
    return pending[0][:quarter] + total + sum(received[1:], received[0])


def contract_rows(left, right):
    return lax.dot_general(
        left, right, (((0,), (0,)), ((), ())), preferred_element_type=jnp.float32
    )


def contract_cols(left, right):
    return lax.dot_general(
        left, right, (((1,), (1,)), ((), ())), preferred_element_type=jnp.float32
    )


def stacked_heads(ref, c):
    return jnp.concatenate(
        [
            ref[:, h * HEAD_SIZE:(h + 1) * HEAD_SIZE]
            for h in range(c * GROUP_HEADS, (c + 1) * GROUP_HEADS)
        ],
        axis=0,
    )


def attention_kernel(
    q_ref, do_ref, kva_ref, kvb_ref, ks_ref, vs_ref, vis_ref, self_ref, live_ref,
    dq_ref, keep_ref, send_ref, sk_ref, sv_ref,
):
    token_rows = q_ref.shape[0]
    width = KEY_HEADS * HEAD_SIZE
    half = kva_ref.shape[0]
    doc_rows = 2 * half
    score_scale = HEAD_SIZE ** (-0.5)
    seen = jnp.concatenate(
        [jnp.concatenate([vis_ref[...], self_ref[...]], axis=0)] * GROUP_HEADS, axis=1
    ) > 0.5
    live = jnp.concatenate([live_ref[...]] * GROUP_HEADS, axis=1)
    for c in range(KEY_HEADS):
        columns = slice(c * HEAD_SIZE, (c + 1) * HEAD_SIZE)
        value_columns = slice(width + c * HEAD_SIZE, width + (c + 1) * HEAD_SIZE)
        keys = jnp.concatenate(
            [kva_ref[:, columns], kvb_ref[:, columns], ks_ref[:, columns]], axis=0
        )
        values = jnp.concatenate(
            [kva_ref[:, value_columns], kvb_ref[:, value_columns], vs_ref[:, columns]], axis=0
        )
        q = stacked_heads(q_ref, c)
        do = stacked_heads(do_ref, c)
        score = jnp.where(seen, contract_cols(keys, q) * score_scale, masked_score)
        top = jnp.max(score, axis=0, keepdims=True)
        grown = jnp.exp(score - top)
        prob = grown * (live / jnp.sum(grown, axis=0, keepdims=True))
        slope = contract_cols(values, do)
        drift = jnp.sum(prob * slope, axis=0, keepdims=True)
        dscore = (prob * (slope - drift)).astype(jnp.bfloat16)
        dq = contract_rows(dscore, keys) * score_scale
        for g in range(GROUP_HEADS):
            h = c * GROUP_HEADS + g
            dq_ref[:, h * HEAD_SIZE:(h + 1) * HEAD_SIZE] = dq[
                g * token_rows:(g + 1) * token_rows
            ].astype(dq_ref.dtype)
        key_total = jnp.dot(dscore, q, preferred_element_type=jnp.float32) * score_scale
        value_total = jnp.dot(prob.astype(jnp.bfloat16), do, preferred_element_type=jnp.float32)
        keep_ref[:, columns] = key_total[:half]
        send_ref[:, columns] = key_total[half:doc_rows].astype(send_ref.dtype)
        keep_ref[:, value_columns] = value_total[:half]
        send_ref[:, value_columns] = value_total[half:doc_rows].astype(send_ref.dtype)
        sk_ref[:, columns] = key_total[doc_rows:].astype(sk_ref.dtype)
        sv_ref[:, columns] = value_total[doc_rows:].astype(sv_ref.dtype)


def per_device(
    queries,
    response_keys,
    response_values,
    document_keys,
    document_values,
    grad_out,
    lengths,
    doc_mask,
):
    token_rows = queries.shape[0]
    responses_here = lengths.shape[0]
    resp_len = token_rows // responses_here
    mask_blocks = doc_mask.shape[1]
    key_value_width = KEY_HEADS * HEAD_SIZE
    positions = jnp.arange(token_rows, dtype=jnp.int32)
    owners = positions // resp_len
    within = positions % resp_len
    live = (within < jnp.repeat(lengths, resp_len)).astype(jnp.float32)[None, :]
    spots = np.arange(token_rows)
    holders_here = spots // resp_len
    self_visible = jnp.asarray(
        (holders_here[:, None] == holders_here[None, :]) & (spots[:, None] <= spots[None, :]),
        jnp.float32,
    )
    size = lax.axis_size("resp")
    doc_mine, doc_other = gather_rows(
        jnp.concatenate([document_keys, document_values], axis=1), "resp"
    )
    slab_rows = document_keys.shape[0]
    doc_rows = size * slab_rows
    half_rows = doc_rows // 2
    block_rows = doc_rows // mask_blocks
    holders = jnp.bitwise_xor(
        lax.axis_index("resp"), jnp.asarray(np.repeat(exchange_pattern(size), slab_rows), jnp.int32)
    )
    global_rows = holders * slab_rows + jnp.asarray(np.tile(np.arange(slab_rows), size), jnp.int32)
    row_masks = jnp.repeat(doc_mask, resp_len, axis=0)
    doc_visible = (jnp.take(row_masks.T, global_rows // block_rows, axis=0) == 1).astype(
        jnp.float32
    )
    query_gradient, doc_keep, doc_send, self_key, self_value = pl.pallas_call(
        attention_kernel,
        out_shape=(
            jax.ShapeDtypeStruct(queries.shape, jnp.bfloat16),
            jax.ShapeDtypeStruct((half_rows, 2 * key_value_width), jnp.float32),
            jax.ShapeDtypeStruct((half_rows, 2 * key_value_width), jnp.bfloat16),
            jax.ShapeDtypeStruct(response_keys.shape, jnp.bfloat16),
            jax.ShapeDtypeStruct(response_values.shape, jnp.bfloat16),
        ),
    )(
        queries,
        grad_out,
        doc_mine,
        doc_other,
        response_keys,
        response_values,
        doc_visible,
        self_visible,
        live,
    )
    summed = scatter_sum_rows(doc_keep, doc_send, "resp")
    return (
        query_gradient,
        summed[:, :key_value_width].astype(jnp.bfloat16),
        summed[:, key_value_width:].astype(jnp.bfloat16),
        self_key,
        self_value,
    )


def solution(mesh):
    return jax.shard_map(
        per_device,
        mesh=mesh,
        in_specs=(
            P(("grp", "resp"), None),
            P(("grp", "resp"), None),
            P(("grp", "resp"), None),
            P(("grp", "resp"), None),
            P(("grp", "resp"), None),
            P(("grp", "resp"), None),
            P(("grp", "resp")),
            P(("grp", "resp"), None),
        ),
        out_specs=(
            P(("grp", "resp"), None),
            P(("grp", "resp"), None),
            P(("grp", "resp"), None),
            P(("grp", "resp"), None),
            P(("grp", "resp"), None),
        ),
        check_vma=False,
    )
```

```python
import jax
import numpy as np
import jax.numpy as jnp
from jax import lax
from jax.experimental import pallas as pl
from jax.sharding import PartitionSpec as P

KEY_HEADS = 4
GROUP_HEADS = 5
HEAD_SIZE = 128


masked_score = -1e30


def exchange_bits(size):
    bits = size.bit_length() - 1
    if (1 << bits) != size:
        return None
    return bits


def swap_with(block, axis_name, size, bit):
    pairs = [(index, index ^ (1 << bit)) for index in range(size)]
    return lax.ppermute(block, axis_name, pairs)


def exchange_sequence(bits):
    order = list(reversed(range(bits)))
    if bits >= 3:
        order[-3], order[-2] = order[-2], order[-3]
    return order


def exchange_pattern(size):
    order = exchange_sequence(exchange_bits(size))
    return [
        sum(((spot >> step) & 1) << bit for step, bit in enumerate(order)) for spot in range(size)
    ]


def gather_rows(blocks, axis_name):
    size = lax.axis_size(axis_name)
    bits = exchange_bits(size)
    halves = None
    for bit in exchange_sequence(bits):
        if halves is not None:
            blocks = jnp.concatenate(halves)
        halves = (blocks, swap_with(blocks, axis_name, size, bit))
    return halves


def scatter_sum_rows(keep, send, axis_name):
    size = lax.axis_size(axis_name)
    bits = exchange_bits(size)
    pending = [keep]
    for step, bit in enumerate(reversed(exchange_sequence(bits))):
        if step > 0:
            split = pending[0].shape[0] // 2
            send = sum(part[split:] for part in pending[1:])
            send = (pending[0][split:] + send).astype(jnp.bfloat16)
            pending = [part[:split] for part in pending]
        pending.append(swap_with(send, axis_name, size, bit).astype(jnp.float32))
    return sum(pending[1:], pending[0])


def contract_rows(left, right):
    return lax.dot_general(
        left, right, (((0,), (0,)), ((), ())), preferred_element_type=jnp.float32
    )


def contract_cols(left, right):
    return lax.dot_general(
        left, right, (((1,), (1,)), ((), ())), preferred_element_type=jnp.float32
    )


def stacked_heads(ref, c):
    return jnp.concatenate(
        [
            ref[:, h * HEAD_SIZE:(h + 1) * HEAD_SIZE]
            for h in range(c * GROUP_HEADS, (c + 1) * GROUP_HEADS)
        ],
        axis=0,
    )


def attention_kernel(
    q_ref, do_ref, kva_ref, kvb_ref, ks_ref, vs_ref, bias_ref, live_ref,
    dq_ref, keep_ref, send_ref, sk_ref, sv_ref,
):
    token_rows = q_ref.shape[0]
    width = KEY_HEADS * HEAD_SIZE
    half = kva_ref.shape[0]
    doc_rows = 2 * half
    score_scale = HEAD_SIZE ** (-0.5)
    live = jnp.concatenate([live_ref[...]] * GROUP_HEADS, axis=1)
    for c in range(KEY_HEADS):
        columns = slice(c * HEAD_SIZE, (c + 1) * HEAD_SIZE)
        value_columns = slice(width + c * HEAD_SIZE, width + (c + 1) * HEAD_SIZE)
        keys = jnp.concatenate(
            [kva_ref[:, columns], kvb_ref[:, columns], ks_ref[:, columns]], axis=0
        )
        values = jnp.concatenate(
            [kva_ref[:, value_columns], kvb_ref[:, value_columns], vs_ref[:, columns]], axis=0
        )
        q = stacked_heads(q_ref, c)
        do = stacked_heads(do_ref, c)
        score = contract_cols(keys, q) * score_scale + bias_ref[...]
        top = jnp.max(score, axis=0, keepdims=True)
        grown = jnp.exp(score - top)
        prob = grown * (live / jnp.sum(grown, axis=0, keepdims=True))
        slope = contract_cols(values, do)
        drift = jnp.sum(prob * slope, axis=0, keepdims=True)
        dscore = (prob * (slope - drift)).astype(jnp.bfloat16)
        dq = contract_rows(dscore, keys) * score_scale
        for g in range(GROUP_HEADS):
            h = c * GROUP_HEADS + g
            dq_ref[:, h * HEAD_SIZE:(h + 1) * HEAD_SIZE] = dq[
                g * token_rows:(g + 1) * token_rows
            ].astype(dq_ref.dtype)
        key_total = jnp.dot(dscore, q, preferred_element_type=jnp.float32) * score_scale
        value_total = jnp.dot(prob.astype(jnp.bfloat16), do, preferred_element_type=jnp.float32)
        keep_ref[:, columns] = key_total[:half]
        send_ref[:, columns] = key_total[half:doc_rows].astype(send_ref.dtype)
        keep_ref[:, value_columns] = value_total[:half]
        send_ref[:, value_columns] = value_total[half:doc_rows].astype(send_ref.dtype)
        sk_ref[:, columns] = key_total[doc_rows:].astype(sk_ref.dtype)
        sv_ref[:, columns] = value_total[doc_rows:].astype(sv_ref.dtype)


def per_device(
    queries,
    response_keys,
    response_values,
    document_keys,
    document_values,
    grad_out,
    lengths,
    doc_mask,
):
    token_rows = queries.shape[0]
    responses_here = lengths.shape[0]
    resp_len = token_rows // responses_here
    mask_blocks = doc_mask.shape[1]
    key_value_width = KEY_HEADS * HEAD_SIZE
    positions = jnp.arange(token_rows, dtype=jnp.int32)
    owners = positions // resp_len
    within = positions % resp_len
    live = (within < jnp.repeat(lengths, resp_len)).astype(jnp.float32)[None, :]
    spots = np.arange(token_rows)
    holders_here = spots // resp_len
    self_visible = jnp.asarray(
        (holders_here[:, None] == holders_here[None, :]) & (spots[:, None] <= spots[None, :]),
        jnp.float32,
    )
    size = lax.axis_size("resp")
    doc_mine, doc_other = gather_rows(
        jnp.concatenate([document_keys, document_values], axis=1), "resp"
    )
    slab_rows = document_keys.shape[0]
    doc_rows = size * slab_rows
    half_rows = doc_rows // 2
    block_rows = doc_rows // mask_blocks
    holders = jnp.bitwise_xor(
        lax.axis_index("resp"), jnp.asarray(np.repeat(exchange_pattern(size), slab_rows), jnp.int32)
    )
    global_rows = holders * slab_rows + jnp.asarray(np.tile(np.arange(slab_rows), size), jnp.int32)
    row_masks = jnp.repeat(doc_mask, resp_len, axis=0)
    doc_visible = (jnp.take(row_masks.T, global_rows // block_rows, axis=0) == 1).astype(
        jnp.float32
    )
    query_gradient, doc_keep, doc_send, self_key, self_value = pl.pallas_call(
        attention_kernel,
        out_shape=(
            jax.ShapeDtypeStruct(queries.shape, jnp.bfloat16),
            jax.ShapeDtypeStruct((half_rows, 2 * key_value_width), jnp.float32),
            jax.ShapeDtypeStruct((half_rows, 2 * key_value_width), jnp.bfloat16),
            jax.ShapeDtypeStruct(response_keys.shape, jnp.bfloat16),
            jax.ShapeDtypeStruct(response_values.shape, jnp.bfloat16),
        ),
    )(
        queries,
        grad_out,
        doc_mine,
        doc_other,
        response_keys,
        response_values,
        jnp.concatenate(
            [jnp.where(jnp.concatenate([doc_visible, self_visible]) > 0.5, 0.0, masked_score)]
            * GROUP_HEADS,
            axis=1,
        ),
        live,
    )
    summed = scatter_sum_rows(doc_keep, doc_send, "resp")
    return (
        query_gradient,
        summed[:, :key_value_width].astype(jnp.bfloat16),
        summed[:, key_value_width:].astype(jnp.bfloat16),
        self_key,
        self_value,
    )


def solution(mesh):
    return jax.shard_map(
        per_device,
        mesh=mesh,
        in_specs=(
            P(("grp", "resp"), None),
            P(("grp", "resp"), None),
            P(("grp", "resp"), None),
            P(("grp", "resp"), None),
            P(("grp", "resp"), None),
            P(("grp", "resp"), None),
            P(("grp", "resp")),
            P(("grp", "resp"), None),
        ),
        out_specs=(
            P(("grp", "resp"), None),
            P(("grp", "resp"), None),
            P(("grp", "resp"), None),
            P(("grp", "resp"), None),
            P(("grp", "resp"), None),
        ),
        check_vma=False,
    )
```

```python
import jax
import numpy as np
import jax.numpy as jnp
from jax import lax
from jax.experimental import pallas as pl
from jax.sharding import PartitionSpec as P

KEY_HEADS = 4
GROUP_HEADS = 5
HEAD_SIZE = 128


masked_score = -1e30


def exchange_bits(size):
    bits = size.bit_length() - 1
    if (1 << bits) != size:
        return None
    return bits


def swap_with(block, axis_name, size, bit):
    pairs = [(index, index ^ (1 << bit)) for index in range(size)]
    return lax.ppermute(block, axis_name, pairs)


def exchange_sequence(bits):
    order = list(reversed(range(bits)))
    if bits >= 3:
        order[-3], order[-2] = order[-2], order[-3]
    return order


def exchange_pattern(size):
    order = exchange_sequence(exchange_bits(size))
    return [
        sum(((spot >> step) & 1) << bit for step, bit in enumerate(order)) for spot in range(size)
    ]


def gather_rows(blocks, axis_name):
    size = lax.axis_size(axis_name)
    bits = exchange_bits(size)
    halves = None
    for bit in exchange_sequence(bits):
        if halves is not None:
            blocks = jnp.concatenate(halves)
        halves = (blocks, swap_with(blocks, axis_name, size, bit))
    return halves


def scatter_sum_rows(keep, send, axis_name):
    size = lax.axis_size(axis_name)
    bits = exchange_bits(size)
    pending = [keep]
    for step, bit in enumerate(reversed(exchange_sequence(bits))):
        if step > 0:
            split = pending[0].shape[0] // 2
            send = sum(part[split:] for part in pending[1:])
            send = (pending[0][split:] + send).astype(jnp.bfloat16)
            pending = [part[:split] for part in pending]
        pending.append(swap_with(send, axis_name, size, bit).astype(jnp.float32))
    return sum(pending[1:], pending[0])


def contract_rows(left, right):
    return lax.dot_general(
        left, right, (((0,), (0,)), ((), ())), preferred_element_type=jnp.float32
    )


def contract_cols(left, right):
    return lax.dot_general(
        left, right, (((1,), (1,)), ((), ())), preferred_element_type=jnp.float32
    )


def stacked_heads(ref, c):
    return jnp.concatenate(
        [
            ref[:, h * HEAD_SIZE:(h + 1) * HEAD_SIZE]
            for h in range(c * GROUP_HEADS, (c + 1) * GROUP_HEADS)
        ],
        axis=0,
    )


def attention_kernel(
    q_ref, do_ref, kva_ref, kvb_ref, ks_ref, vs_ref, vis_ref, self_ref, live_ref,
    dq_ref, keep_ref, send_ref, sk_ref, sv_ref,
):
    token_rows = q_ref.shape[1] // GROUP_HEADS
    width = KEY_HEADS * HEAD_SIZE
    half = kva_ref.shape[0]
    doc_rows = 2 * half
    score_scale = HEAD_SIZE ** (-0.5)
    seen = jnp.concatenate(
        [jnp.concatenate([vis_ref[...], self_ref[...]], axis=0)] * GROUP_HEADS, axis=1
    ) > 0.5
    live = jnp.concatenate([live_ref[...]] * GROUP_HEADS, axis=1)
    for c in range(KEY_HEADS):
        columns = slice(c * HEAD_SIZE, (c + 1) * HEAD_SIZE)
        value_columns = slice(width + c * HEAD_SIZE, width + (c + 1) * HEAD_SIZE)
        keys = jnp.concatenate(
            [kva_ref[:, columns], kvb_ref[:, columns], ks_ref[:, columns]], axis=0
        )
        values = jnp.concatenate(
            [kva_ref[:, value_columns], kvb_ref[:, value_columns], vs_ref[:, columns]], axis=0
        )
        q = q_ref[c]
        do = do_ref[c]
        score = jnp.where(seen, contract_cols(keys, q) * score_scale, masked_score)
        top = jnp.max(score, axis=0, keepdims=True)
        grown = jnp.exp(score - top)
        prob = grown * (live / jnp.sum(grown, axis=0, keepdims=True))
        slope = contract_cols(values, do)
        drift = jnp.sum(prob * slope, axis=0, keepdims=True)
        dscore = (prob * (slope - drift)).astype(jnp.bfloat16)
        dq = contract_rows(dscore, keys) * score_scale
        for g in range(GROUP_HEADS):
            h = c * GROUP_HEADS + g
            dq_ref[:, h * HEAD_SIZE:(h + 1) * HEAD_SIZE] = dq[
                g * token_rows:(g + 1) * token_rows
            ].astype(dq_ref.dtype)
        key_total = jnp.dot(dscore, q, preferred_element_type=jnp.float32) * score_scale
        value_total = jnp.dot(prob.astype(jnp.bfloat16), do, preferred_element_type=jnp.float32)
        keep_ref[:, columns] = key_total[:half]
        send_ref[:, columns] = key_total[half:doc_rows].astype(send_ref.dtype)
        keep_ref[:, value_columns] = value_total[:half]
        send_ref[:, value_columns] = value_total[half:doc_rows].astype(send_ref.dtype)
        sk_ref[:, columns] = key_total[doc_rows:].astype(sk_ref.dtype)
        sv_ref[:, columns] = value_total[doc_rows:].astype(sv_ref.dtype)


def per_device(
    queries,
    response_keys,
    response_values,
    document_keys,
    document_values,
    grad_out,
    lengths,
    doc_mask,
):
    token_rows = queries.shape[0]
    responses_here = lengths.shape[0]
    resp_len = token_rows // responses_here
    mask_blocks = doc_mask.shape[1]
    key_value_width = KEY_HEADS * HEAD_SIZE
    positions = jnp.arange(token_rows, dtype=jnp.int32)
    owners = positions // resp_len
    within = positions % resp_len
    live = (within < jnp.repeat(lengths, resp_len)).astype(jnp.float32)[None, :]
    spots = np.arange(token_rows)
    holders_here = spots // resp_len
    self_visible = jnp.asarray(
        (holders_here[:, None] == holders_here[None, :]) & (spots[:, None] <= spots[None, :]),
        jnp.float32,
    )
    size = lax.axis_size("resp")
    doc_mine, doc_other = gather_rows(
        jnp.concatenate([document_keys, document_values], axis=1), "resp"
    )
    slab_rows = document_keys.shape[0]
    doc_rows = size * slab_rows
    half_rows = doc_rows // 2
    block_rows = doc_rows // mask_blocks
    holders = jnp.bitwise_xor(
        lax.axis_index("resp"), jnp.asarray(np.repeat(exchange_pattern(size), slab_rows), jnp.int32)
    )
    global_rows = holders * slab_rows + jnp.asarray(np.tile(np.arange(slab_rows), size), jnp.int32)
    row_masks = jnp.repeat(doc_mask, resp_len, axis=0)
    doc_visible = (jnp.take(row_masks.T, global_rows // block_rows, axis=0) == 1).astype(
        jnp.float32
    )
    query_gradient, doc_keep, doc_send, self_key, self_value = pl.pallas_call(
        attention_kernel,
        out_shape=(
            jax.ShapeDtypeStruct(queries.shape, jnp.bfloat16),
            jax.ShapeDtypeStruct((half_rows, 2 * key_value_width), jnp.float32),
            jax.ShapeDtypeStruct((half_rows, 2 * key_value_width), jnp.bfloat16),
            jax.ShapeDtypeStruct(response_keys.shape, jnp.bfloat16),
            jax.ShapeDtypeStruct(response_values.shape, jnp.bfloat16),
        ),
    )(
        jnp.transpose(
            queries.reshape(token_rows, KEY_HEADS, GROUP_HEADS, HEAD_SIZE), (1, 2, 0, 3)
        ).reshape(KEY_HEADS, GROUP_HEADS * token_rows, HEAD_SIZE),
        jnp.transpose(
            grad_out.reshape(token_rows, KEY_HEADS, GROUP_HEADS, HEAD_SIZE), (1, 2, 0, 3)
        ).reshape(KEY_HEADS, GROUP_HEADS * token_rows, HEAD_SIZE),
        doc_mine,
        doc_other,
        response_keys,
        response_values,
        doc_visible,
        self_visible,
        live,
    )
    summed = scatter_sum_rows(doc_keep, doc_send, "resp")
    return (
        query_gradient,
        summed[:, :key_value_width].astype(jnp.bfloat16),
        summed[:, key_value_width:].astype(jnp.bfloat16),
        self_key,
        self_value,
    )


def solution(mesh):
    return jax.shard_map(
        per_device,
        mesh=mesh,
        in_specs=(
            P(("grp", "resp"), None),
            P(("grp", "resp"), None),
            P(("grp", "resp"), None),
            P(("grp", "resp"), None),
            P(("grp", "resp"), None),
            P(("grp", "resp"), None),
            P(("grp", "resp")),
            P(("grp", "resp"), None),
        ),
        out_specs=(
            P(("grp", "resp"), None),
            P(("grp", "resp"), None),
            P(("grp", "resp"), None),
            P(("grp", "resp"), None),
            P(("grp", "resp"), None),
        ),
        check_vma=False,
    )
```

```python
import jax
import numpy as np
import jax.numpy as jnp
from jax import lax
from jax.experimental import pallas as pl
from jax.sharding import PartitionSpec as P

KEY_HEADS = 4
GROUP_HEADS = 5
HEAD_SIZE = 128


masked_score = -1e30


def exchange_bits(size):
    bits = size.bit_length() - 1
    if (1 << bits) != size:
        return None
    return bits


def swap_with(block, axis_name, size, bit):
    pairs = [(index, index ^ (1 << bit)) for index in range(size)]
    return lax.ppermute(block, axis_name, pairs)


def exchange_sequence(bits):
    order = list(reversed(range(bits)))
    if bits >= 3:
        order[-3], order[-2] = order[-2], order[-3]
    return order


def exchange_pattern(size):
    order = exchange_sequence(exchange_bits(size))
    return [
        sum(((spot >> step) & 1) << bit for step, bit in enumerate(order)) for spot in range(size)
    ]


def gather_rows(blocks, axis_name):
    size = lax.axis_size(axis_name)
    bits = exchange_bits(size)
    halves = None
    for bit in exchange_sequence(bits):
        if halves is not None:
            blocks = jnp.concatenate(halves)
        halves = (blocks, swap_with(blocks, axis_name, size, bit))
    return halves


def scatter_sum_rows(keep, send, axis_name):
    size = lax.axis_size(axis_name)
    bits = exchange_bits(size)
    pending = [keep]
    for step, bit in enumerate(reversed(exchange_sequence(bits))):
        if step > 0:
            split = pending[0].shape[0] // 2
            send = sum(part[split:] for part in pending[1:])
            send = (pending[0][split:] + send).astype(jnp.bfloat16)
            pending = [part[:split] for part in pending]
        pending.append(swap_with(send, axis_name, size, bit).astype(jnp.float32))
    return sum(pending[1:], pending[0])


def contract_rows(left, right):
    return lax.dot_general(
        left, right, (((0,), (0,)), ((), ())), preferred_element_type=jnp.float32
    )


def contract_cols(left, right):
    return lax.dot_general(
        left, right, (((1,), (1,)), ((), ())), preferred_element_type=jnp.float32
    )


def stacked_heads(ref, c):
    return jnp.concatenate(
        [
            ref[:, h * HEAD_SIZE:(h + 1) * HEAD_SIZE]
            for h in range(c * GROUP_HEADS, (c + 1) * GROUP_HEADS)
        ],
        axis=0,
    )


def attention_kernel(
    q_ref, do_ref, kva_ref, kvb_ref, ks_ref, vs_ref, seen_ref, live_ref,
    dq_ref, keep_ref, send_ref, sk_ref, sv_ref,
):
    token_rows = q_ref.shape[0]
    width = KEY_HEADS * HEAD_SIZE
    half = kva_ref.shape[0]
    doc_rows = 2 * half
    score_scale = HEAD_SIZE ** (-0.5)
    seen = jnp.concatenate([seen_ref[...]] * GROUP_HEADS, axis=1) > 0.5
    live = jnp.concatenate([live_ref[...]] * GROUP_HEADS, axis=1)
    for c in range(KEY_HEADS):
        columns = slice(c * HEAD_SIZE, (c + 1) * HEAD_SIZE)
        value_columns = slice(width + c * HEAD_SIZE, width + (c + 1) * HEAD_SIZE)
        keys = jnp.concatenate(
            [kva_ref[:, columns], kvb_ref[:, columns], ks_ref[:, columns]], axis=0
        )
        values = jnp.concatenate(
            [kva_ref[:, value_columns], kvb_ref[:, value_columns], vs_ref[:, columns]], axis=0
        )
        q = stacked_heads(q_ref, c)
        do = stacked_heads(do_ref, c)
        score = jnp.where(seen, contract_cols(keys, q) * score_scale, masked_score)
        top = jnp.max(score, axis=0, keepdims=True)
        grown = jnp.exp(score - top)
        prob = grown * (live / jnp.sum(grown, axis=0, keepdims=True))
        slope = contract_cols(values, do)
        drift = jnp.sum(prob * slope, axis=0, keepdims=True)
        dscore = (prob * (slope - drift)).astype(jnp.bfloat16)
        dq = contract_rows(dscore, keys) * score_scale
        for g in range(GROUP_HEADS):
            h = c * GROUP_HEADS + g
            dq_ref[:, h * HEAD_SIZE:(h + 1) * HEAD_SIZE] = dq[
                g * token_rows:(g + 1) * token_rows
            ].astype(dq_ref.dtype)
        key_total = jnp.dot(dscore, q, preferred_element_type=jnp.float32) * score_scale
        value_total = jnp.dot(prob.astype(jnp.bfloat16), do, preferred_element_type=jnp.float32)
        keep_ref[:, columns] = key_total[:half]
        send_ref[:, columns] = key_total[half:doc_rows].astype(send_ref.dtype)
        keep_ref[:, value_columns] = value_total[:half]
        send_ref[:, value_columns] = value_total[half:doc_rows].astype(send_ref.dtype)
        sk_ref[:, columns] = key_total[doc_rows:].astype(sk_ref.dtype)
        sv_ref[:, columns] = value_total[doc_rows:].astype(sv_ref.dtype)


def per_device(
    queries,
    response_keys,
    response_values,
    document_keys,
    document_values,
    grad_out,
    lengths,
    doc_mask,
):
    token_rows = queries.shape[0]
    responses_here = lengths.shape[0]
    resp_len = token_rows // responses_here
    mask_blocks = doc_mask.shape[1]
    key_value_width = KEY_HEADS * HEAD_SIZE
    positions = jnp.arange(token_rows, dtype=jnp.int32)
    owners = positions // resp_len
    within = positions % resp_len
    live = (within < jnp.repeat(lengths, resp_len)).astype(jnp.float32)[None, :]
    spots = np.arange(token_rows)
    holders_here = spots // resp_len
    self_visible = jnp.asarray(
        (holders_here[:, None] == holders_here[None, :]) & (spots[:, None] <= spots[None, :]),
        jnp.float32,
    )
    size = lax.axis_size("resp")
    doc_mine, doc_other = gather_rows(
        jnp.concatenate([document_keys, document_values], axis=1), "resp"
    )
    slab_rows = document_keys.shape[0]
    doc_rows = size * slab_rows
    half_rows = doc_rows // 2
    block_rows = doc_rows // mask_blocks
    holders = jnp.bitwise_xor(
        lax.axis_index("resp"), jnp.asarray(np.repeat(exchange_pattern(size), slab_rows), jnp.int32)
    )
    global_rows = holders * slab_rows + jnp.asarray(np.tile(np.arange(slab_rows), size), jnp.int32)
    row_masks = jnp.repeat(doc_mask, resp_len, axis=0)
    doc_visible = (jnp.take(row_masks.T, global_rows // block_rows, axis=0) == 1).astype(
        jnp.float32
    )
    query_gradient, doc_keep, doc_send, self_key, self_value = pl.pallas_call(
        attention_kernel,
        out_shape=(
            jax.ShapeDtypeStruct(queries.shape, jnp.bfloat16),
            jax.ShapeDtypeStruct((half_rows, 2 * key_value_width), jnp.float32),
            jax.ShapeDtypeStruct((half_rows, 2 * key_value_width), jnp.bfloat16),
            jax.ShapeDtypeStruct(response_keys.shape, jnp.bfloat16),
            jax.ShapeDtypeStruct(response_values.shape, jnp.bfloat16),
        ),
    )(
        queries,
        grad_out,
        doc_mine,
        doc_other,
        response_keys,
        response_values,
        jnp.concatenate([doc_visible, self_visible]),
        live,
    )
    summed = scatter_sum_rows(doc_keep, doc_send, "resp")
    return (
        query_gradient,
        summed[:, :key_value_width].astype(jnp.bfloat16),
        summed[:, key_value_width:].astype(jnp.bfloat16),
        self_key,
        self_value,
    )


def solution(mesh):
    return jax.shard_map(
        per_device,
        mesh=mesh,
        in_specs=(
            P(("grp", "resp"), None),
            P(("grp", "resp"), None),
            P(("grp", "resp"), None),
            P(("grp", "resp"), None),
            P(("grp", "resp"), None),
            P(("grp", "resp"), None),
            P(("grp", "resp")),
            P(("grp", "resp"), None),
        ),
        out_specs=(
            P(("grp", "resp"), None),
            P(("grp", "resp"), None),
            P(("grp", "resp"), None),
            P(("grp", "resp"), None),
            P(("grp", "resp"), None),
        ),
        check_vma=False,
    )
```
